512 devices in a mesh: blk: 64 (over y_lo, z, core), uly: 8 (over y_hi, x).
Axes of the slice: x: 4, y: 8 (y_hi: 2, y_lo: 4; y = y_hi * 4 + y_lo), z: 8, core: 2. Of those that a mesh axis runs over, the one named last changes fastest.
Arguments:
- query: bfloat16 [65536, 3072], P(('blk', 'uly')), may hold values from -40 to 40
- keys: bfloat16 [65536, 3072], P(('blk', 'uly')), may hold values from -5.2 to 5.2
- values: bfloat16 [65536, 3072], P(('blk', 'uly')), may hold values from -5 to 5
- block_mask: int32 [512, 512], P('blk'), may hold values from 0 to 1, as said below
Outputs:
- grad_query: bfloat16 [65536, 3072], P(('blk', 'uly'))
- grad_keys: bfloat16 [65536, 3072], P(('blk', 'uly'))
- grad_values: bfloat16 [65536, 3072], P(('blk', 'uly'))
The draws below stay inside these ranges and needn't reach their ends.
Inputs may be any that keep to these rules, and one draw needn't show every extreme that they name: block_mask is symmetric, its diagonal is all ones, it is zero wherever |i - j| > 8, and each row holds at most 5 ones, some rows exactly 5.
All inputs are finite; a program needn't handle non-finite values.
Results may differ from the reference program's by a relative error of at most 0.017.
Values may be sent and summed in bfloat16 or wider, within the bound.
No kernel may reach another device: no remote copies, remote signals or barrier semaphores. Data moves between devices by JAX's collectives and lax.ppermute only.
A program may use at most 128 MiB of HBM per device.

```python
import jax
import jax.numpy as jnp
from jax import lax

HD = 128
HEADS = 24
BLK = 128
M = 5
BPD = 8
TOKENS = 65536
NB = 512


def paired_draw(key):
    first, second = jax.random.split(jax.random.fold_in(key, 4099), 2)
    shape = (TOKENS, HEADS * HD)
    query = jax.random.truncated_normal(first, -5.0, 5.0, shape, jnp.float32)
    keys = jax.random.truncated_normal(second, -5.0, 5.0, shape, jnp.float32)
    return (query, keys)


def draw_query(key, part):
    return paired_draw(key)[0].astype(jnp.bfloat16)


def draw_keys(key, part):
    return paired_draw(key)[1].astype(jnp.bfloat16)


def draw_block_mask(key, part):
    first, second = jax.random.split(jax.random.fold_in(key, 77))
    farthest = jax.random.randint(first, (), 2, BPD + 1)
    row_ids = jnp.arange(NB)[:, None]
    col_ids = jnp.arange(NB)[None, :]
    spacing = jnp.abs(col_ids - row_ids)
    lower = jnp.minimum(row_ids, col_ids)
    keep_table = jax.random.randint(second, (NB, BPD + 1), 0, 5)
    kept = keep_table[lower, jnp.minimum(spacing, BPD)] < 3
    forced = lower // (4 * BPD) % 4 == 0
    offsets = (spacing == 1) | (spacing == farthest)
    allowed = (spacing == 0) | offsets & (kept | forced)
    return allowed.astype(jnp.int32)


def levels(own_key, dims, pieces, smallest, top_value):
    gain = 1.0
    for dim, shards_of in pieces:
        steps = jax.random.uniform(jax.random.fold_in(jax.random.fold_in(own_key, 6), dim), (shards_of,), jnp.float32, smallest / len(pieces), top_value / len(pieces))
        gain = gain * jnp.repeat(jnp.exp(steps), dims[dim] // shards_of).reshape((-1,) + (1,) * (len(dims) - 1 - dim))
    return gain


def centred(stream_key, dims, spread, limit, cuts=(), kind=jnp.bfloat16):
    level = levels(stream_key, dims, cuts, -0.22, 0.18) if cuts else 1.0
    entries = jax.random.normal(stream_key, dims, jnp.float32) * spread * level
    return jnp.minimum(jnp.maximum(entries, -limit), limit).astype(kind)


def setup_inputs(seed: int = 0) -> dict:
    arg_keys = jax.random.split(jax.random.key(seed), 5)
    return {
        "query": draw_query(jax.random.fold_in(arg_keys[4], 71), 0),
        "keys": draw_keys(jax.random.fold_in(arg_keys[4], 71), 0),
        "values": centred(arg_keys[2], (TOKENS, HEADS * HD), 1.0, 5.0, ((0, 512),)),
        "block_mask": draw_block_mask(jax.random.fold_in(arg_keys[4], 71), 0),
    }


loss_scale = 64.0
masked = -1.0e30


def block_lists(rows, count):
    width = rows.shape[-1]
    running = jnp.cumsum(rows, axis=-1).astype(jnp.int32)
    ranks = jnp.arange(1, count + 1, dtype=jnp.int32)
    hits = (rows[..., None, :] == 1) & (running[..., None, :] == ranks[:, None])
    columns = jnp.arange(width, dtype=jnp.int32)
    slot_index = jnp.sum(jnp.where(hits, columns, 0), axis=-1).astype(jnp.int32)
    slot_valid = jnp.any(hits, axis=-1)
    return slot_index, slot_valid


def round_half(array):
    return lax.optimization_barrier(array.astype(jnp.bfloat16)).astype(jnp.float32)


def reference(query, keys, values, block_mask):
    scale = HD ** -0.5
    nblocks = TOKENS // BLK
    query_blocks = query.reshape(nblocks, BLK, HEADS, HD)
    key_blocks = keys.reshape(nblocks, BLK, HEADS, HD)
    value_blocks = values.reshape(nblocks, BLK, HEADS, HD)
    slot_index, slot_valid = block_lists(block_mask, M)

    def forward(block):
        chosen = slot_index[block]
        usable = slot_valid[block]
        query_one = query_blocks[block].astype(jnp.float32)
        key_tiles = key_blocks[chosen].astype(jnp.float32)
        value_tiles = value_blocks[chosen].astype(jnp.float32)
        scores = jnp.einsum('thd,muhd->htmu', query_one, key_tiles) * scale
        scores = jnp.where(usable[None, None, :, None], scores, masked)
        row_top = jnp.max(scores, axis=(2, 3))
        log_total = row_top + jnp.log(jnp.sum(jnp.exp(scores - row_top[:, :, None, None]), axis=(2, 3)))
        weights = jnp.exp(scores - log_total[:, :, None, None])
        weights_b = round_half(weights)
        attended = jnp.einsum('htmu,muhd->thd', weights_b, value_tiles)
        grad_out = (loss_scale * attended).astype(jnp.bfloat16)
        grad_float = grad_out.astype(jnp.float32)
        row_delta = jnp.transpose(jnp.sum(grad_float * attended, axis=2))
        grad_weights = jnp.einsum('thd,muhd->htmu', grad_float, value_tiles)
        grad_scores = weights * (grad_weights - row_delta[:, :, None, None])
        grad_scores_b = round_half(grad_scores)
        grad_one = (jnp.einsum('htmu,muhd->thd', grad_scores_b, key_tiles) * scale).astype(jnp.bfloat16)
        return grad_one, grad_out, log_total, row_delta

    grad_query, grad_outs, log_totals, row_deltas = lax.map(forward, jnp.arange(nblocks, dtype=jnp.int32))

    def backward(block):
        chosen = slot_index[block]
        usable = slot_valid[block]
        query_tiles = query_blocks[chosen].astype(jnp.float32)
        grad_tiles = grad_outs[chosen].astype(jnp.float32)
        total_tiles = log_totals[chosen]
        delta_tiles = row_deltas[chosen]
        key_one = key_blocks[block].astype(jnp.float32)
        value_one = value_blocks[block].astype(jnp.float32)
        scores = jnp.einsum('mthd,uhd->mhtu', query_tiles, key_one) * scale
        weights = jnp.where(usable[:, None, None, None], jnp.exp(scores - total_tiles[..., None]), 0.0)
        weights_b = round_half(weights)
        grad_value_one = jnp.einsum('mhtu,mthd->uhd', weights_b, grad_tiles).astype(jnp.bfloat16)
        grad_weights = jnp.einsum('mthd,uhd->mhtu', grad_tiles, value_one)
        grad_scores = weights * (grad_weights - delta_tiles[..., None])
        grad_scores_b = round_half(grad_scores)
        grad_key_one = (jnp.einsum('mhtu,mthd->uhd', grad_scores_b, query_tiles) * scale).astype(jnp.bfloat16)
        return grad_key_one, grad_value_one

    grad_keys, grad_values = lax.map(backward, jnp.arange(nblocks, dtype=jnp.int32))
    width = HEADS * HD
    return (grad_query.reshape(TOKENS, width), grad_keys.reshape(TOKENS, width), grad_values.reshape(TOKENS, width))
```

```python
import jax
import jax.numpy as jnp
from jax import lax
from jax.sharding import PartitionSpec as P

HD = 128
BLK = 128
M = 5


loss_scale = 64.0
masked = -1e30


def padded(cells, sides, width):
    for axis, dim in sides:
        count = lax.axis_size(axis)
        ends = count - 1
        head = lax.slice_in_dim(cells, 0, width, axis=dim)
        tail = lax.slice_in_dim(cells, cells.shape[dim] - width, cells.shape[dim], axis=dim)
        cells = jnp.concatenate(
            [
                lax.ppermute(tail, axis, [(i, (i + 1) % count) for i in range(ends)]),
                cells,
                lax.ppermute(head, axis, [((i + 1) % count, i) for i in range(ends)]),
            ],
            axis=dim,
        )
    return cells


def from_behind(value, axis, steps):
    count = lax.axis_size(axis)
    initial, last = (max(0, -steps), min(count, count - steps))
    return lax.ppermute(value, axis, [(source, source + steps) for source in range(initial, last)])


def block_lists(rows, count):
    width = rows.shape[-1]
    running = jnp.cumsum(rows, axis=-1)
    ranks = jnp.arange(1, count + 1, dtype=jnp.int32)
    hits = (rows[..., None, :] == 1) & (running[..., None, :] == ranks[:, None])
    columns = jnp.arange(width, dtype=jnp.int32)
    slot_index = jnp.sum(jnp.where(hits, columns, 0), axis=-1)
    slot_valid = jnp.any(hits, axis=-1)
    return (slot_index, slot_valid)


def attend_rows(query_one, key_window, value_window, slot_index, slot_valid, scale):
    key_tiles = key_window[slot_index]
    value_tiles = value_window[slot_index]
    scores = (
        jnp.einsum("rtd,rmud->rtmu", query_one, key_tiles, preferred_element_type=jnp.float32)
        * scale
    )
    scores = jnp.where(slot_valid[:, None, :, None], scores, masked)
    row_top = jnp.max(scores, axis=(2, 3))
    log_total = row_top + jnp.log(jnp.sum(jnp.exp(scores - row_top[:, :, None, None]), axis=(2, 3)))
    weights = jnp.exp(scores - log_total[:, :, None, None])
    weights_b = weights.astype(jnp.bfloat16)
    attended = jnp.einsum(
        "rtmu,rmud->rtd", weights_b, value_tiles, preferred_element_type=jnp.float32
    )
    grad_out = (loss_scale * attended).astype(jnp.bfloat16)
    row_delta = jnp.sum(grad_out.astype(jnp.float32) * attended, axis=2)
    grad_weights = jnp.einsum(
        "rtd,rmud->rtmu", grad_out, value_tiles, preferred_element_type=jnp.float32
    )
    grad_scores = weights * (grad_weights - row_delta[:, :, None, None])
    grad_scores_b = grad_scores.astype(jnp.bfloat16)
    grad_one = (
        jnp.einsum("rtmu,rmud->rtd", grad_scores_b, key_tiles, preferred_element_type=jnp.float32)
        * scale
    ).astype(jnp.bfloat16)
    return (grad_one, grad_out, log_total, row_delta, weights_b, grad_scores_b)


def one_head(query_one, key_win, value_win, slot_index, slot_valid, scale):
    grad_one, grad_out, log_total, row_delta, weights_b, grad_scores_b = attend_rows(
        query_one, key_win, value_win, slot_index, slot_valid, scale
    )
    value_part = jnp.einsum(
        "rtmu,rtd->rmud", weights_b, grad_out, preferred_element_type=jnp.float32
    )
    key_part = (
        jnp.einsum(
            "rtmu,rtd->rmud", grad_scores_b, query_one, preferred_element_type=jnp.float32
        )
        * scale
    )
    slots = key_win.shape[0]
    picks = (slot_index[:, :, None] == jnp.arange(slots, dtype=slot_index.dtype)) & slot_valid[
        :, :, None
    ]
    picks = picks.astype(jnp.float32)
    key_slots = jnp.einsum("rmw,rmud->wud", picks, key_part, precision=lax.Precision.HIGHEST)
    value_slots = jnp.einsum("rmw,rmud->wud", picks, value_part, precision=lax.Precision.HIGHEST)
    return (grad_one, key_slots, value_slots)


def body(query, keys, values, block_mask):
    scale = HD ** (-0.5)
    tokens_here = query.shape[0]
    heads_all = query.shape[1] // HD
    spread = lax.axis_size("uly")
    heads_here = heads_all // spread
    group_tokens = tokens_here * spread
    group_blocks = group_tokens // BLK
    position = lax.axis_index("blk")
    padded_mask = jnp.pad(block_mask, ((0, 0), (group_blocks, group_blocks)))
    window_mask = lax.dynamic_slice_in_dim(
        padded_mask, position * group_blocks, 3 * group_blocks, 1
    )
    slot_index, slot_valid = block_lists(window_mask, M)

    def pick(array, h):
        split = array.reshape(tokens_here, spread, heads_here, HD)[:, :, h, :]
        return jnp.transpose(split, (1, 0, 2))

    results = []
    for h in range(heads_here):
        with jax.named_scope(f"head{h}"):
            sent = jnp.stack([pick(query, h), pick(keys, h), pick(values, h)])
            got = lax.all_to_all(sent, "uly", split_axis=1, concat_axis=1, tiled=True)
            got = got.reshape(3, group_tokens, HD)
            beside = padded(got[1:], (("blk", 1),), group_tokens)
            key_window = beside[0].reshape(3 * group_blocks, BLK, HD)
            value_window = beside[1].reshape(3 * group_blocks, BLK, HD)
            query_blocks = got[0].reshape(group_blocks, BLK, HD)
            grad_one, key_slots, value_slots = one_head(
                query_blocks, key_window, value_window, slot_index, slot_valid, scale
            )
            slot_sums = jnp.stack([key_slots, value_slots]).reshape(2, 3 * group_tokens, HD)
            from_upper = from_behind(
                slot_sums[:, :group_tokens].astype(jnp.bfloat16), "blk", -1
            ).astype(jnp.float32)
            from_lower = from_behind(
                slot_sums[:, 2 * group_tokens :].astype(jnp.bfloat16), "blk", 1
            ).astype(jnp.float32)
            totals = slot_sums[:, group_tokens : 2 * group_tokens] + from_upper + from_lower
            grads = jnp.concatenate(
                [grad_one.reshape(1, group_tokens, HD), totals.astype(jnp.bfloat16)]
            )
            grads = grads.reshape(3, spread, tokens_here, HD)
            back = lax.all_to_all(grads, "uly", split_axis=1, concat_axis=1, tiled=True)
            results.append(back)
    stacked = jnp.stack(results)
    stacked = jnp.transpose(stacked, (1, 3, 2, 0, 4)).reshape(3, tokens_here, heads_all * HD)
    return (stacked[0], stacked[1], stacked[2])


def solution(mesh):
    in_specs = (
        P(("blk", "uly"), None),
        P(("blk", "uly"), None),
        P(("blk", "uly"), None),
        P("blk", None),
    )
    out_specs = (P(("blk", "uly"), None), P(("blk", "uly"), None), P(("blk", "uly"), None))
    return jax.shard_map(body, mesh=mesh, in_specs=in_specs, out_specs=out_specs, check_vma=False)
```

```python
import jax
import jax.numpy as jnp
from jax import lax
from jax.sharding import PartitionSpec as P

HD = 128
BLK = 128
M = 5


loss_scale = 64.0
masked = -1e30


def padded(cells, sides, width):
    for axis, dim in sides:
        count = lax.axis_size(axis)
        ends = count - 1
        head = lax.slice_in_dim(cells, 0, width, axis=dim)
        tail = lax.slice_in_dim(cells, cells.shape[dim] - width, cells.shape[dim], axis=dim)
        cells = jnp.concatenate(
            [
                lax.ppermute(tail, axis, [(i, (i + 1) % count) for i in range(ends)]),
                cells,
                lax.ppermute(head, axis, [((i + 1) % count, i) for i in range(ends)]),
            ],
            axis=dim,
        )
    return cells


def from_behind(value, axis, steps):
    count = lax.axis_size(axis)
    initial, last = (max(0, -steps), min(count, count - steps))
    return lax.ppermute(value, axis, [(source, source + steps) for source in range(initial, last)])


def block_lists(rows, count):
    width = rows.shape[-1]
    running = jnp.cumsum(rows, axis=-1)
    ranks = jnp.arange(1, count + 1, dtype=jnp.int32)
    hits = (rows[..., None, :] == 1) & (running[..., None, :] == ranks[:, None])
    columns = jnp.arange(width, dtype=jnp.int32)
    slot_index = jnp.sum(jnp.where(hits, columns, 0), axis=-1)
    slot_valid = jnp.any(hits, axis=-1)
    return (slot_index, slot_valid)


def attend_rows(query_one, key_window, value_window, slot_index, slot_valid, scale):
    key_tiles = key_window[slot_index]
    value_tiles = value_window[slot_index]
    scores = (
        jnp.einsum("rtd,rmud->rtmu", query_one, key_tiles, preferred_element_type=jnp.float32)
        * scale
    )
    scores = jnp.where(slot_valid[:, None, :, None], scores, masked)
    row_top = jnp.max(scores, axis=(2, 3))
    log_total = row_top + jnp.log(jnp.sum(jnp.exp(scores - row_top[:, :, None, None]), axis=(2, 3)))
    weights = jnp.exp(scores - log_total[:, :, None, None])
    weights_b = weights.astype(jnp.bfloat16)
    attended = jnp.einsum(
        "rtmu,rmud->rtd", weights_b, value_tiles, preferred_element_type=jnp.float32
    )
    grad_out = (loss_scale * attended).astype(jnp.bfloat16)
    row_delta = jnp.sum(grad_out.astype(jnp.float32) * attended, axis=2)
    grad_weights = jnp.einsum(
        "rtd,rmud->rtmu", grad_out, value_tiles, preferred_element_type=jnp.float32
    )
    grad_scores = weights * (grad_weights - row_delta[:, :, None, None])
    grad_scores_b = grad_scores.astype(jnp.bfloat16)
    grad_one = (
        jnp.einsum("rtmu,rmud->rtd", grad_scores_b, key_tiles, preferred_element_type=jnp.float32)
        * scale
    ).astype(jnp.bfloat16)
    return (grad_one, grad_out, log_total, row_delta, weights_b, grad_scores_b)


def one_head(query_one, key_win, value_win, slot_index, slot_valid, scale):
    grad_one, grad_out, log_total, row_delta, weights_b, grad_scores_b = attend_rows(
        query_one, key_win, value_win, slot_index, slot_valid, scale
    )
    value_part = jnp.einsum(
        "rtmu,rtd->rmud", weights_b, grad_out, preferred_element_type=jnp.float32
    )
    key_part = (
        jnp.einsum(
            "rtmu,rtd->rmud", grad_scores_b, query_one, preferred_element_type=jnp.float32
        )
        * scale
    )
    slots = key_win.shape[0]
    picks = (slot_index[:, :, None] == jnp.arange(slots, dtype=slot_index.dtype)) & slot_valid[
        :, :, None
    ]
    picks = picks.astype(jnp.float32)
    key_slots = jnp.einsum("rmw,rmud->wud", picks, key_part, precision=lax.Precision.HIGHEST)
    value_slots = jnp.einsum("rmw,rmud->wud", picks, value_part, precision=lax.Precision.HIGHEST)
    return (grad_one, key_slots, value_slots)


def body(query, keys, values, block_mask):
    scale = HD ** (-0.5)
    tokens_here = query.shape[0]
    heads_all = query.shape[1] // HD
    spread = lax.axis_size("uly")
    heads_here = heads_all // spread
    group_tokens = tokens_here * spread
    group_blocks = group_tokens // BLK
    position = lax.axis_index("blk")
    padded_mask = jnp.pad(block_mask, ((0, 0), (group_blocks, group_blocks)))
    window_mask = lax.dynamic_slice_in_dim(
        padded_mask, position * group_blocks, 3 * group_blocks, 1
    )
    slot_index, slot_valid = block_lists(window_mask, M)

    def pick(array, h):
        split = array.reshape(tokens_here, spread, heads_here, HD)[:, :, h, :]
        return jnp.transpose(split, (1, 0, 2))

    sends = []
    for h in range(heads_here):
        with jax.named_scope(f"head{h}"):
            sends.append(jnp.stack([pick(query, h), pick(keys, h), pick(values, h)]))
    gots = []
    for h in range(heads_here):
        with jax.named_scope(f"head{h}"):
            sent = sends[h]
            if h > 0:
                sent, _ = lax.optimization_barrier((sent, gots[h - 1]))
            gots.append(lax.all_to_all(sent, "uly", split_axis=1, concat_axis=1, tiled=True))
    results = []
    last = None
    for h in range(heads_here):
        with jax.named_scope(f"head{h}"):
            got = gots[h]
            if last is not None:
                got, _ = lax.optimization_barrier((got, last))
            got = got.reshape(3, group_tokens, HD)
            beside = padded(got[1:], (("blk", 1),), group_tokens)
            key_window = beside[0].reshape(3 * group_blocks, BLK, HD)
            value_window = beside[1].reshape(3 * group_blocks, BLK, HD)
            query_blocks = got[0].reshape(group_blocks, BLK, HD)
            grad_one, key_slots, value_slots = one_head(
                query_blocks, key_window, value_window, slot_index, slot_valid, scale
            )
            slot_sums = jnp.stack([key_slots, value_slots]).reshape(2, 3 * group_tokens, HD)
            from_upper = from_behind(
                slot_sums[:, :group_tokens].astype(jnp.bfloat16), "blk", -1
            ).astype(jnp.float32)
            from_lower = from_behind(
                slot_sums[:, 2 * group_tokens :].astype(jnp.bfloat16), "blk", 1
            ).astype(jnp.float32)
            last = grad_one
            totals = slot_sums[:, group_tokens : 2 * group_tokens] + from_upper + from_lower
            grads = jnp.concatenate(
                [grad_one.reshape(1, group_tokens, HD), totals.astype(jnp.bfloat16)]
            )
            grads = grads.reshape(3, spread, tokens_here, HD)
            if h + 2 < heads_here:
                grads, _ = lax.optimization_barrier((grads, gots[h + 2]))
            back = lax.all_to_all(grads, "uly", split_axis=1, concat_axis=1, tiled=True)
            results.append(back)
    stacked = jnp.stack(results)
    stacked = jnp.transpose(stacked, (1, 3, 2, 0, 4)).reshape(3, tokens_here, heads_all * HD)
    return (stacked[0], stacked[1], stacked[2])


def solution(mesh):
    in_specs = (
        P(("blk", "uly"), None),
        P(("blk", "uly"), None),
        P(("blk", "uly"), None),
        P("blk", None),
    )
    out_specs = (P(("blk", "uly"), None), P(("blk", "uly"), None), P(("blk", "uly"), None))
    return jax.shard_map(body, mesh=mesh, in_specs=in_specs, out_specs=out_specs, check_vma=False)
```

```python
import jax
import jax.numpy as jnp
from jax import lax
from jax.sharding import PartitionSpec as P
from jax.experimental import pallas as pl
from jax.experimental.pallas import tpu as pltpu
import functools

HD = 128
BLK = 128
M = 5


loss_scale = 64.0
masked = -1e30


def padded(cells, sides, width):
    for axis, dim in sides:
        count = lax.axis_size(axis)
        ends = count - 1
        head = lax.slice_in_dim(cells, 0, width, axis=dim)
        tail = lax.slice_in_dim(cells, cells.shape[dim] - width, cells.shape[dim], axis=dim)
        cells = jnp.concatenate(
            [
                lax.ppermute(tail, axis, [(i, (i + 1) % count) for i in range(ends)]),
                cells,
                lax.ppermute(head, axis, [((i + 1) % count, i) for i in range(ends)]),
            ],
            axis=dim,
        )
    return cells


def from_behind(value, axis, steps):
    count = lax.axis_size(axis)
    initial, last = (max(0, -steps), min(count, count - steps))
    return lax.ppermute(value, axis, [(source, source + steps) for source in range(initial, last)])


def block_lists(rows, count):
    width = rows.shape[-1]
    running = jnp.cumsum(rows, axis=-1)
    ranks = jnp.arange(1, count + 1, dtype=jnp.int32)
    hits = (rows[..., None, :] == 1) & (running[..., None, :] == ranks[:, None])
    columns = jnp.arange(width, dtype=jnp.int32)
    slot_index = jnp.sum(jnp.where(hits, columns, 0), axis=-1)
    slot_valid = jnp.any(hits, axis=-1)
    return (slot_index, slot_valid)


def attend_rows(query_one, key_window, value_window, slot_index, slot_valid, scale):
    key_tiles = key_window[slot_index]
    value_tiles = value_window[slot_index]
    scores = (
        jnp.einsum("rtd,rmud->rtmu", query_one, key_tiles, preferred_element_type=jnp.float32)
        * scale
    )
    scores = jnp.where(slot_valid[:, None, :, None], scores, masked)
    row_top = jnp.max(scores, axis=(2, 3))
    log_total = row_top + jnp.log(jnp.sum(jnp.exp(scores - row_top[:, :, None, None]), axis=(2, 3)))
    weights = jnp.exp(scores - log_total[:, :, None, None])
    weights_b = weights.astype(jnp.bfloat16)
    attended = jnp.einsum(
        "rtmu,rmud->rtd", weights_b, value_tiles, preferred_element_type=jnp.float32
    )
    grad_out = (loss_scale * attended).astype(jnp.bfloat16)
    row_delta = jnp.sum(grad_out.astype(jnp.float32) * attended, axis=2)
    grad_weights = jnp.einsum(
        "rtd,rmud->rtmu", grad_out, value_tiles, preferred_element_type=jnp.float32
    )
    grad_scores = weights * (grad_weights - row_delta[:, :, None, None])
    grad_scores_b = grad_scores.astype(jnp.bfloat16)
    grad_one = (
        jnp.einsum("rtmu,rmud->rtd", grad_scores_b, key_tiles, preferred_element_type=jnp.float32)
        * scale
    ).astype(jnp.bfloat16)
    return (grad_one, grad_out, log_total, row_delta, weights_b, grad_scores_b)


def one_head(query_one, key_win, value_win, slot_index, slot_valid, scale):
    grad_one, grad_out, log_total, row_delta, weights_b, grad_scores_b = attend_rows(
        query_one, key_win, value_win, slot_index, slot_valid, scale
    )
    value_part = jnp.einsum(
        "rtmu,rtd->rmud", weights_b, grad_out, preferred_element_type=jnp.float32
    )
    key_part = (
        jnp.einsum(
            "rtmu,rtd->rmud", grad_scores_b, query_one, preferred_element_type=jnp.float32
        )
        * scale
    )
    slots = key_win.shape[0]
    picks = (slot_index[:, :, None] == jnp.arange(slots, dtype=slot_index.dtype)) & slot_valid[
        :, :, None
    ]
    picks = picks.astype(jnp.float32)
    key_slots = jnp.einsum("rmw,rmud->wud", picks, key_part, precision=lax.Precision.HIGHEST)
    value_slots = jnp.einsum("rmw,rmud->wud", picks, value_part, precision=lax.Precision.HIGHEST)
    return (grad_one, key_slots, value_slots)


def head_kernel(idx_ref, valid_ref, q_ref, kw_ref, vw_ref, gq_ref, ks_ref, vs_ref, *, scale):
    r = pl.program_id(0)

    @pl.when(r == 0)
    def _():
        ks_ref[...] = jnp.zeros(ks_ref.shape, ks_ref.dtype)
        vs_ref[...] = jnp.zeros(vs_ref.shape, vs_ref.dtype)

    q = q_ref[0]
    slots = [idx_ref[r * M + m] for m in range(M)]
    flags = [valid_ref[r * M + m] > 0 for m in range(M)]
    ks = [kw_ref[s] for s in slots]
    vs = [vw_ref[s] for s in slots]
    nt = (((1,), (1,)), ((), ()))
    tn = (((0,), (0,)), ((), ()))
    scores = []
    for m in range(M):
        s = lax.dot_general(q, ks[m], nt, preferred_element_type=jnp.float32) * scale
        scores.append(jnp.where(flags[m], s, masked))
    top = scores[0].max(axis=1, keepdims=True)
    for m in range(1, M):
        top = jnp.maximum(top, scores[m].max(axis=1, keepdims=True))
    total = jnp.zeros_like(top)
    for m in range(M):
        total = total + jnp.exp(scores[m] - top).sum(axis=1, keepdims=True)
    log_total = top + jnp.log(total)
    weights = [jnp.exp(s - log_total) for s in scores]
    weights_b = [w.astype(jnp.bfloat16) for w in weights]
    attended = jnp.zeros((BLK, HD), jnp.float32)
    for m in range(M):
        attended = attended + jnp.dot(weights_b[m], vs[m], preferred_element_type=jnp.float32)
    grad_out = (loss_scale * attended).astype(jnp.bfloat16)
    row_delta = (grad_out.astype(jnp.float32) * attended).sum(axis=1, keepdims=True)
    grad_q = jnp.zeros((BLK, HD), jnp.float32)
    for m in range(M):
        grad_w = lax.dot_general(grad_out, vs[m], nt, preferred_element_type=jnp.float32)
        grad_s = (weights[m] * (grad_w - row_delta)).astype(jnp.bfloat16)
        grad_q = grad_q + jnp.dot(grad_s, ks[m], preferred_element_type=jnp.float32)
        key_part = lax.dot_general(grad_s, q, tn, preferred_element_type=jnp.float32) * scale
        value_part = lax.dot_general(weights_b[m], grad_out, tn, preferred_element_type=jnp.float32)
        keep = jnp.where(flags[m], 1.0, 0.0)
        ks_ref[slots[m]] = ks_ref[slots[m]] + key_part * keep
        vs_ref[slots[m]] = vs_ref[slots[m]] + value_part * keep
    gq_ref[0] = (grad_q * scale).astype(gq_ref.dtype)


def head_call(query_blocks, key_window, value_window, slot_index, slot_valid, scale):
    rows = query_blocks.shape[0]
    width = key_window.shape[0]
    idx = slot_index.reshape(-1).astype(jnp.int32)
    val = slot_valid.reshape(-1).astype(jnp.int32)
    whole = lambda r, i, v: (0, 0, 0)
    own = lambda r, i, v: (r, 0, 0)
    spec = pltpu.PrefetchScalarGridSpec(
        num_scalar_prefetch=2,
        grid=(rows,),
        in_specs=[
            pl.BlockSpec((1, BLK, HD), own),
            pl.BlockSpec((width, BLK, HD), whole),
            pl.BlockSpec((width, BLK, HD), whole),
        ],
        out_specs=[
            pl.BlockSpec((1, BLK, HD), own),
            pl.BlockSpec((width, BLK, HD), whole),
            pl.BlockSpec((width, BLK, HD), whole),
        ],
    )
    return pl.pallas_call(
        functools.partial(head_kernel, scale=scale),
        grid_spec=spec,
        out_shape=[
            jax.ShapeDtypeStruct((rows, BLK, HD), jnp.bfloat16),
            jax.ShapeDtypeStruct((width, BLK, HD), jnp.float32),
            jax.ShapeDtypeStruct((width, BLK, HD), jnp.float32),
        ],
        compiler_params=pltpu.CompilerParams(dimension_semantics=("arbitrary",)),
    )(idx, val, query_blocks, key_window, value_window)


def body(query, keys, values, block_mask):
    scale = HD ** (-0.5)
    tokens_here = query.shape[0]
    heads_all = query.shape[1] // HD
    spread = lax.axis_size("uly")
    heads_here = heads_all // spread
    group_tokens = tokens_here * spread
    group_blocks = group_tokens // BLK
    position = lax.axis_index("blk")
    padded_mask = jnp.pad(block_mask, ((0, 0), (group_blocks, group_blocks)))
    window_mask = lax.dynamic_slice_in_dim(
        padded_mask, position * group_blocks, 3 * group_blocks, 1
    )
    slot_index, slot_valid = block_lists(window_mask, M)

    def pick(array, h):
        split = array.reshape(tokens_here, spread, heads_here, HD)[:, :, h, :]
        return jnp.transpose(split, (1, 0, 2))

    sends = []
    for h in range(heads_here):
        with jax.named_scope(f"head{h}"):
            sends.append(jnp.stack([pick(query, h), pick(keys, h), pick(values, h)]))
    gots = []
    for h in range(heads_here):
        with jax.named_scope(f"head{h}"):
            sent = sends[h]
            if h > 0:
                sent, _ = lax.optimization_barrier((sent, gots[h - 1]))
            gots.append(lax.all_to_all(sent, "uly", split_axis=1, concat_axis=1, tiled=True))
    results = []
    last = None
    for h in range(heads_here):
        with jax.named_scope(f"head{h}"):
            got = gots[h]
            if last is not None:
                got, _ = lax.optimization_barrier((got, last))
            got = got.reshape(3, group_tokens, HD)
            beside = padded(got[1:], (("blk", 1),), group_tokens)
            key_window = beside[0].reshape(3 * group_blocks, BLK, HD)
            value_window = beside[1].reshape(3 * group_blocks, BLK, HD)
            query_blocks = got[0].reshape(group_blocks, BLK, HD)
            grad_one, key_slots, value_slots = head_call(
                query_blocks, key_window, value_window, slot_index, slot_valid, scale
            )
            slot_sums = jnp.stack([key_slots, value_slots]).reshape(2, 3 * group_tokens, HD)
            from_upper = from_behind(
                slot_sums[:, :group_tokens].astype(jnp.bfloat16), "blk", -1
            ).astype(jnp.float32)
            from_lower = from_behind(
                slot_sums[:, 2 * group_tokens :].astype(jnp.bfloat16), "blk", 1
            ).astype(jnp.float32)
            last = grad_one
            totals = slot_sums[:, group_tokens : 2 * group_tokens] + from_upper + from_lower
            grads = jnp.concatenate(
                [grad_one.reshape(1, group_tokens, HD), totals.astype(jnp.bfloat16)]
            )
            grads = grads.reshape(3, spread, tokens_here, HD)
            if h + 2 < heads_here:
                grads, _ = lax.optimization_barrier((grads, gots[h + 2]))
            back = lax.all_to_all(grads, "uly", split_axis=1, concat_axis=1, tiled=True)
            results.append(back)
    stacked = jnp.stack(results)
    stacked = jnp.transpose(stacked, (1, 3, 2, 0, 4)).reshape(3, tokens_here, heads_all * HD)
    return (stacked[0], stacked[1], stacked[2])


def solution(mesh):
    in_specs = (
        P(("blk", "uly"), None),
        P(("blk", "uly"), None),
        P(("blk", "uly"), None),
        P("blk", None),
    )
    out_specs = (P(("blk", "uly"), None), P(("blk", "uly"), None), P(("blk", "uly"), None))
    return jax.shard_map(body, mesh=mesh, in_specs=in_specs, out_specs=out_specs, check_vma=False)
```

```python
import jax
import jax.numpy as jnp
from jax import lax
from jax.sharding import PartitionSpec as P
from jax.experimental import pallas as pl
from jax.experimental.pallas import tpu as pltpu
import functools

HD = 128
BLK = 128
M = 5


loss_scale = 64.0
masked = -1e30


def padded(cells, sides, width):
    for axis, dim in sides:
        count = lax.axis_size(axis)
        ends = count - 1
        head = lax.slice_in_dim(cells, 0, width, axis=dim)
        tail = lax.slice_in_dim(cells, cells.shape[dim] - width, cells.shape[dim], axis=dim)
        cells = jnp.concatenate(
            [
                lax.ppermute(tail, axis, [(i, (i + 1) % count) for i in range(ends)]),
                cells,
                lax.ppermute(head, axis, [((i + 1) % count, i) for i in range(ends)]),
            ],
            axis=dim,
        )
    return cells


def from_behind(value, axis, steps):
    count = lax.axis_size(axis)
    initial, last = (max(0, -steps), min(count, count - steps))
    return lax.ppermute(value, axis, [(source, source + steps) for source in range(initial, last)])


def block_lists(rows, count):
    width = rows.shape[-1]
    running = jnp.cumsum(rows, axis=-1)
    ranks = jnp.arange(1, count + 1, dtype=jnp.int32)
    hits = (rows[..., None, :] == 1) & (running[..., None, :] == ranks[:, None])
    columns = jnp.arange(width, dtype=jnp.int32)
    slot_index = jnp.sum(jnp.where(hits, columns, 0), axis=-1)
    slot_valid = jnp.any(hits, axis=-1)
    return (slot_index, slot_valid)


def attend_rows(query_one, key_window, value_window, slot_index, slot_valid, scale):
    key_tiles = key_window[slot_index]
    value_tiles = value_window[slot_index]
    scores = (
        jnp.einsum("rtd,rmud->rtmu", query_one, key_tiles, preferred_element_type=jnp.float32)
        * scale
    )
    scores = jnp.where(slot_valid[:, None, :, None], scores, masked)
    row_top = jnp.max(scores, axis=(2, 3))
    log_total = row_top + jnp.log(jnp.sum(jnp.exp(scores - row_top[:, :, None, None]), axis=(2, 3)))
    weights = jnp.exp(scores - log_total[:, :, None, None])
    weights_b = weights.astype(jnp.bfloat16)
    attended = jnp.einsum(
        "rtmu,rmud->rtd", weights_b, value_tiles, preferred_element_type=jnp.float32
    )
    grad_out = (loss_scale * attended).astype(jnp.bfloat16)
    row_delta = jnp.sum(grad_out.astype(jnp.float32) * attended, axis=2)
    grad_weights = jnp.einsum(
        "rtd,rmud->rtmu", grad_out, value_tiles, preferred_element_type=jnp.float32
    )
    grad_scores = weights * (grad_weights - row_delta[:, :, None, None])
    grad_scores_b = grad_scores.astype(jnp.bfloat16)
    grad_one = (
        jnp.einsum("rtmu,rmud->rtd", grad_scores_b, key_tiles, preferred_element_type=jnp.float32)
        * scale
    ).astype(jnp.bfloat16)
    return (grad_one, grad_out, log_total, row_delta, weights_b, grad_scores_b)


def one_head(query_one, key_win, value_win, slot_index, slot_valid, scale):
    grad_one, grad_out, log_total, row_delta, weights_b, grad_scores_b = attend_rows(
        query_one, key_win, value_win, slot_index, slot_valid, scale
    )
    value_part = jnp.einsum(
        "rtmu,rtd->rmud", weights_b, grad_out, preferred_element_type=jnp.float32
    )
    key_part = (
        jnp.einsum(
            "rtmu,rtd->rmud", grad_scores_b, query_one, preferred_element_type=jnp.float32
        )
        * scale
    )
    slots = key_win.shape[0]
    picks = (slot_index[:, :, None] == jnp.arange(slots, dtype=slot_index.dtype)) & slot_valid[
        :, :, None
    ]
    picks = picks.astype(jnp.float32)
    key_slots = jnp.einsum("rmw,rmud->wud", picks, key_part, precision=lax.Precision.HIGHEST)
    value_slots = jnp.einsum("rmw,rmud->wud", picks, value_part, precision=lax.Precision.HIGHEST)
    return (grad_one, key_slots, value_slots)


def head_kernel(idx_ref, valid_ref, q_ref, kw_ref, vw_ref, gq_ref, ks_ref, vs_ref, *, scale):
    r = pl.program_id(1)

    @pl.when(r == 0)
    def _():
        ks_ref[...] = jnp.zeros(ks_ref.shape, ks_ref.dtype)
        vs_ref[...] = jnp.zeros(vs_ref.shape, vs_ref.dtype)

    q = q_ref[0, 0]
    slots = [idx_ref[r * M + m] for m in range(M)]
    flags = [valid_ref[r * M + m] > 0 for m in range(M)]
    ks = [kw_ref[0, s] for s in slots]
    vs = [vw_ref[0, s] for s in slots]
    nt = (((1,), (1,)), ((), ()))
    tn = (((0,), (0,)), ((), ()))
    scores = []
    for m in range(M):
        s = lax.dot_general(q, ks[m], nt, preferred_element_type=jnp.float32) * scale
        scores.append(jnp.where(flags[m], s, masked))
    top = scores[0].max(axis=1, keepdims=True)
    for m in range(1, M):
        top = jnp.maximum(top, scores[m].max(axis=1, keepdims=True))
    total = jnp.zeros_like(top)
    for m in range(M):
        total = total + jnp.exp(scores[m] - top).sum(axis=1, keepdims=True)
    log_total = top + jnp.log(total)
    weights = [jnp.exp(s - log_total) for s in scores]
    weights_b = [w.astype(jnp.bfloat16) for w in weights]
    attended = jnp.zeros((BLK, HD), jnp.float32)
    for m in range(M):
        attended = attended + jnp.dot(weights_b[m], vs[m], preferred_element_type=jnp.float32)
    grad_out = (loss_scale * attended).astype(jnp.bfloat16)
    row_delta = (grad_out.astype(jnp.float32) * attended).sum(axis=1, keepdims=True)
    grad_q = jnp.zeros((BLK, HD), jnp.float32)
    for m in range(M):
        grad_w = lax.dot_general(grad_out, vs[m], nt, preferred_element_type=jnp.float32)
        grad_s = (weights[m] * (grad_w - row_delta)).astype(jnp.bfloat16)
        grad_q = grad_q + jnp.dot(grad_s, ks[m], preferred_element_type=jnp.float32)
        key_part = lax.dot_general(grad_s, q, tn, preferred_element_type=jnp.float32) * scale
        value_part = lax.dot_general(weights_b[m], grad_out, tn, preferred_element_type=jnp.float32)
        keep = jnp.where(flags[m], 1.0, 0.0)
        ks_ref[0, slots[m]] = ks_ref[0, slots[m]] + key_part * keep
        vs_ref[0, slots[m]] = vs_ref[0, slots[m]] + value_part * keep
    gq_ref[0, 0] = (grad_q * scale).astype(gq_ref.dtype)


def head_call(query_blocks, key_window, value_window, slot_index, slot_valid, scale):
    heads, rows = query_blocks.shape[:2]
    width = key_window.shape[1]
    idx = slot_index.reshape(-1).astype(jnp.int32)
    val = slot_valid.reshape(-1).astype(jnp.int32)
    whole = lambda h, r, i, v: (h, 0, 0, 0)
    own = lambda h, r, i, v: (h, r, 0, 0)
    spec = pltpu.PrefetchScalarGridSpec(
        num_scalar_prefetch=2,
        grid=(heads, rows),
        in_specs=[
            pl.BlockSpec((1, 1, BLK, HD), own),
            pl.BlockSpec((1, width, BLK, HD), whole),
            pl.BlockSpec((1, width, BLK, HD), whole),
        ],
        out_specs=[
            pl.BlockSpec((1, 1, BLK, HD), own),
            pl.BlockSpec((1, width, BLK, HD), whole),
            pl.BlockSpec((1, width, BLK, HD), whole),
        ],
    )
    return pl.pallas_call(
        functools.partial(head_kernel, scale=scale),
        grid_spec=spec,
        out_shape=[
            jax.ShapeDtypeStruct((heads, rows, BLK, HD), jnp.bfloat16),
            jax.ShapeDtypeStruct((heads, width, BLK, HD), jnp.float32),
            jax.ShapeDtypeStruct((heads, width, BLK, HD), jnp.float32),
        ],
        compiler_params=pltpu.CompilerParams(dimension_semantics=("arbitrary", "arbitrary")),
    )(idx, val, query_blocks, key_window, value_window)


def body(query, keys, values, block_mask):
    scale = HD ** (-0.5)
    tokens_here = query.shape[0]
    heads_all = query.shape[1] // HD
    spread = lax.axis_size("uly")
    heads_here = heads_all // spread
    group_tokens = tokens_here * spread
    group_blocks = group_tokens // BLK
    position = lax.axis_index("blk")
    padded_mask = jnp.pad(block_mask, ((0, 0), (group_blocks, group_blocks)))
    window_mask = lax.dynamic_slice_in_dim(
        padded_mask, position * group_blocks, 3 * group_blocks, 1
    )
    slot_index, slot_valid = block_lists(window_mask, M)

    def heads_major(array):
        split = array.reshape(tokens_here, spread, heads_here, HD)
        return jnp.transpose(split, (2, 1, 0, 3))

    sent = jnp.stack([heads_major(query), heads_major(keys), heads_major(values)])
    got = lax.all_to_all(sent, "uly", split_axis=2, concat_axis=2, tiled=True)
    got = got.reshape(3, heads_here, group_tokens, HD)
    beside = padded(got[1:], (("blk", 2),), group_tokens)
    key_window = beside[0].reshape(heads_here, 3 * group_blocks, BLK, HD)
    value_window = beside[1].reshape(heads_here, 3 * group_blocks, BLK, HD)
    query_blocks = got[0].reshape(heads_here, group_blocks, BLK, HD)
    grad_one, key_slots, value_slots = head_call(
        query_blocks, key_window, value_window, slot_index, slot_valid, scale
    )
    slot_sums = jnp.stack([key_slots, value_slots]).reshape(2, heads_here, 3 * group_tokens, HD)
    from_upper = from_behind(
        slot_sums[:, :, :group_tokens].astype(jnp.bfloat16), "blk", -1
    ).astype(jnp.float32)
    from_lower = from_behind(
        slot_sums[:, :, 2 * group_tokens :].astype(jnp.bfloat16), "blk", 1
    ).astype(jnp.float32)
    totals = slot_sums[:, :, group_tokens : 2 * group_tokens] + from_upper + from_lower
    grads = jnp.concatenate(
        [grad_one.reshape(1, heads_here, group_tokens, HD), totals.astype(jnp.bfloat16)]
    )
    grads = grads.reshape(3, heads_here, spread, tokens_here, HD)
    back = lax.all_to_all(grads, "uly", split_axis=2, concat_axis=2, tiled=True)
    back = jnp.transpose(back, (0, 3, 2, 1, 4)).reshape(3, tokens_here, heads_all * HD)
    return (back[0], back[1], back[2])


def solution(mesh):
    in_specs = (
        P(("blk", "uly"), None),
        P(("blk", "uly"), None),
        P(("blk", "uly"), None),
        P("blk", None),
    )
    out_specs = (P(("blk", "uly"), None), P(("blk", "uly"), None), P(("blk", "uly"), None))
    return jax.shard_map(body, mesh=mesh, in_specs=in_specs, out_specs=out_specs, check_vma=False)
```

```python
import jax
import jax.numpy as jnp
from jax import lax
from jax.sharding import PartitionSpec as P
from jax.experimental import pallas as pl
from jax.experimental.pallas import tpu as pltpu
import functools

HD = 128
BLK = 128
M = 5


loss_scale = 64.0
masked = -1e30


def padded(cells, sides, width):
    for axis, dim in sides:
        count = lax.axis_size(axis)
        ends = count - 1
        head = lax.slice_in_dim(cells, 0, width, axis=dim)
        tail = lax.slice_in_dim(cells, cells.shape[dim] - width, cells.shape[dim], axis=dim)
        cells = jnp.concatenate(
            [
                lax.ppermute(tail, axis, [(i, (i + 1) % count) for i in range(ends)]),
                cells,
                lax.ppermute(head, axis, [((i + 1) % count, i) for i in range(ends)]),
            ],
            axis=dim,
        )
    return cells


def from_behind(value, axis, steps):
    count = lax.axis_size(axis)
    initial, last = (max(0, -steps), min(count, count - steps))
    return lax.ppermute(value, axis, [(source, source + steps) for source in range(initial, last)])


def block_lists(rows, count):
    width = rows.shape[-1]
    running = jnp.cumsum(rows, axis=-1)
    ranks = jnp.arange(1, count + 1, dtype=jnp.int32)
    hits = (rows[..., None, :] == 1) & (running[..., None, :] == ranks[:, None])
    columns = jnp.arange(width, dtype=jnp.int32)
    slot_index = jnp.sum(jnp.where(hits, columns, 0), axis=-1)
    slot_valid = jnp.any(hits, axis=-1)
    return (slot_index, slot_valid)


def attend_rows(query_one, key_window, value_window, slot_index, slot_valid, scale):
    key_tiles = key_window[slot_index]
    value_tiles = value_window[slot_index]
    scores = (
        jnp.einsum("rtd,rmud->rtmu", query_one, key_tiles, preferred_element_type=jnp.float32)
        * scale
    )
    scores = jnp.where(slot_valid[:, None, :, None], scores, masked)
    row_top = jnp.max(scores, axis=(2, 3))
    log_total = row_top + jnp.log(jnp.sum(jnp.exp(scores - row_top[:, :, None, None]), axis=(2, 3)))
    weights = jnp.exp(scores - log_total[:, :, None, None])
    weights_b = weights.astype(jnp.bfloat16)
    attended = jnp.einsum(
        "rtmu,rmud->rtd", weights_b, value_tiles, preferred_element_type=jnp.float32
    )
    grad_out = (loss_scale * attended).astype(jnp.bfloat16)
    row_delta = jnp.sum(grad_out.astype(jnp.float32) * attended, axis=2)
    grad_weights = jnp.einsum(
        "rtd,rmud->rtmu", grad_out, value_tiles, preferred_element_type=jnp.float32
    )
    grad_scores = weights * (grad_weights - row_delta[:, :, None, None])
    grad_scores_b = grad_scores.astype(jnp.bfloat16)
    grad_one = (
        jnp.einsum("rtmu,rmud->rtd", grad_scores_b, key_tiles, preferred_element_type=jnp.float32)
        * scale
    ).astype(jnp.bfloat16)
    return (grad_one, grad_out, log_total, row_delta, weights_b, grad_scores_b)


def one_head(query_one, key_win, value_win, slot_index, slot_valid, scale):
    grad_one, grad_out, log_total, row_delta, weights_b, grad_scores_b = attend_rows(
        query_one, key_win, value_win, slot_index, slot_valid, scale
    )
    value_part = jnp.einsum(
        "rtmu,rtd->rmud", weights_b, grad_out, preferred_element_type=jnp.float32
    )
    key_part = (
        jnp.einsum(
            "rtmu,rtd->rmud", grad_scores_b, query_one, preferred_element_type=jnp.float32
        )
        * scale
    )
    slots = key_win.shape[0]
    picks = (slot_index[:, :, None] == jnp.arange(slots, dtype=slot_index.dtype)) & slot_valid[
        :, :, None
    ]
    picks = picks.astype(jnp.float32)
    key_slots = jnp.einsum("rmw,rmud->wud", picks, key_part, precision=lax.Precision.HIGHEST)
    value_slots = jnp.einsum("rmw,rmud->wud", picks, value_part, precision=lax.Precision.HIGHEST)
    return (grad_one, key_slots, value_slots)


def head_kernel(idx_ref, valid_ref, q_ref, kw_ref, vw_ref, gq_ref, ks_ref, vs_ref, *, scale):
    r = pl.program_id(1)

    @pl.when(r == 0)
    def _():
        ks_ref[...] = jnp.zeros(ks_ref.shape, ks_ref.dtype)
        vs_ref[...] = jnp.zeros(vs_ref.shape, vs_ref.dtype)

    q = q_ref[0, 0]
    slots = [idx_ref[r * M + m] for m in range(M)]
    flags = [valid_ref[r * M + m] > 0 for m in range(M)]
    key_tiles = jnp.concatenate([kw_ref[0, s] for s in slots], axis=0)
    value_tiles = jnp.concatenate([vw_ref[0, s] for s in slots], axis=0)
    nt = (((1,), (1,)), ((), ()))
    tn = (((0,), (0,)), ((), ()))
    column = lax.broadcasted_iota(jnp.int32, (1, M * BLK), 1) // BLK
    usable = column < 0
    for m in range(M):
        usable = usable | ((column == m) & flags[m])
    scores = lax.dot_general(q, key_tiles, nt, preferred_element_type=jnp.float32) * scale
    scores = jnp.where(usable, scores, masked)
    top = scores.max(axis=1, keepdims=True)
    log_total = top + jnp.log(jnp.exp(scores - top).sum(axis=1, keepdims=True))
    weights = jnp.exp(scores - log_total)
    weights_b = weights.astype(jnp.bfloat16)
    attended = jnp.dot(weights_b, value_tiles, preferred_element_type=jnp.float32)
    grad_out = (loss_scale * attended).astype(jnp.bfloat16)
    row_delta = (grad_out.astype(jnp.float32) * attended).sum(axis=1, keepdims=True)
    grad_w = lax.dot_general(grad_out, value_tiles, nt, preferred_element_type=jnp.float32)
    grad_s = (weights * (grad_w - row_delta)).astype(jnp.bfloat16)
    grad_q = jnp.dot(grad_s, key_tiles, preferred_element_type=jnp.float32)
    key_part = lax.dot_general(grad_s, q, tn, preferred_element_type=jnp.float32) * scale
    value_part = lax.dot_general(weights_b, grad_out, tn, preferred_element_type=jnp.float32)
    for m in range(M):
        keep = jnp.where(flags[m], 1.0, 0.0)
        ks_ref[0, slots[m]] = ks_ref[0, slots[m]] + key_part[m * BLK : (m + 1) * BLK] * keep
        vs_ref[0, slots[m]] = vs_ref[0, slots[m]] + value_part[m * BLK : (m + 1) * BLK] * keep
    gq_ref[0, 0] = (grad_q * scale).astype(gq_ref.dtype)


def head_call(query_blocks, key_window, value_window, slot_index, slot_valid, scale):
    heads, rows = query_blocks.shape[:2]
    width = key_window.shape[1]
    idx = slot_index.reshape(-1).astype(jnp.int32)
    val = slot_valid.reshape(-1).astype(jnp.int32)
    whole = lambda h, r, i, v: (h, 0, 0, 0)
    own = lambda h, r, i, v: (h, r, 0, 0)
    spec = pltpu.PrefetchScalarGridSpec(
        num_scalar_prefetch=2,
        grid=(heads, rows),
        in_specs=[
            pl.BlockSpec((1, 1, BLK, HD), own),
            pl.BlockSpec((1, width, BLK, HD), whole),
            pl.BlockSpec((1, width, BLK, HD), whole),
        ],
        out_specs=[
            pl.BlockSpec((1, 1, BLK, HD), own),
            pl.BlockSpec((1, width, BLK, HD), whole),
            pl.BlockSpec((1, width, BLK, HD), whole),
        ],
    )
    return pl.pallas_call(
        functools.partial(head_kernel, scale=scale),
        grid_spec=spec,
        out_shape=[
            jax.ShapeDtypeStruct((heads, rows, BLK, HD), jnp.bfloat16),
            jax.ShapeDtypeStruct((heads, width, BLK, HD), jnp.float32),
            jax.ShapeDtypeStruct((heads, width, BLK, HD), jnp.float32),
        ],
        compiler_params=pltpu.CompilerParams(dimension_semantics=("arbitrary", "arbitrary")),
    )(idx, val, query_blocks, key_window, value_window)


def body(query, keys, values, block_mask):
    scale = HD ** (-0.5)
    tokens_here = query.shape[0]
    heads_all = query.shape[1] // HD
    spread = lax.axis_size("uly")
    heads_here = heads_all // spread
    group_tokens = tokens_here * spread
    group_blocks = group_tokens // BLK
    position = lax.axis_index("blk")
    padded_mask = jnp.pad(block_mask, ((0, 0), (group_blocks, group_blocks)))
    window_mask = lax.dynamic_slice_in_dim(
        padded_mask, position * group_blocks, 3 * group_blocks, 1
    )
    slot_index, slot_valid = block_lists(window_mask, M)

    def heads_major(array):
        split = array.reshape(tokens_here, spread, heads_here, HD)
        return jnp.transpose(split, (2, 1, 0, 3))

    sent = jnp.stack([heads_major(query), heads_major(keys), heads_major(values)])
    got = lax.all_to_all(sent, "uly", split_axis=2, concat_axis=2, tiled=True)
    got = got.reshape(3, heads_here, group_tokens, HD)
    beside = padded(got[1:], (("blk", 2),), group_tokens)
    key_window = beside[0].reshape(heads_here, 3 * group_blocks, BLK, HD)
    value_window = beside[1].reshape(heads_here, 3 * group_blocks, BLK, HD)
    query_blocks = got[0].reshape(heads_here, group_blocks, BLK, HD)
    grad_one, key_slots, value_slots = head_call(
        query_blocks, key_window, value_window, slot_index, slot_valid, scale
    )
    slot_sums = jnp.stack([key_slots, value_slots]).reshape(2, heads_here, 3 * group_tokens, HD)
    from_upper = from_behind(
        slot_sums[:, :, :group_tokens].astype(jnp.bfloat16), "blk", -1
    ).astype(jnp.float32)
    from_lower = from_behind(
        slot_sums[:, :, 2 * group_tokens :].astype(jnp.bfloat16), "blk", 1
    ).astype(jnp.float32)
    totals = slot_sums[:, :, group_tokens : 2 * group_tokens] + from_upper + from_lower
    grads = jnp.concatenate(
        [grad_one.reshape(1, heads_here, group_tokens, HD), totals.astype(jnp.bfloat16)]
    )
    grads = grads.reshape(3, heads_here, spread, tokens_here, HD)
    back = lax.all_to_all(grads, "uly", split_axis=2, concat_axis=2, tiled=True)
    back = jnp.transpose(back, (0, 3, 2, 1, 4)).reshape(3, tokens_here, heads_all * HD)
    return (back[0], back[1], back[2])


def solution(mesh):
    in_specs = (
        P(("blk", "uly"), None),
        P(("blk", "uly"), None),
        P(("blk", "uly"), None),
        P("blk", None),
    )
    out_specs = (P(("blk", "uly"), None), P(("blk", "uly"), None), P(("blk", "uly"), None))
    return jax.shard_map(body, mesh=mesh, in_specs=in_specs, out_specs=out_specs, check_vma=False)
```

```python
import jax
import jax.numpy as jnp
from jax import lax
from jax.sharding import PartitionSpec as P
from jax.experimental import pallas as pl
from jax.experimental.pallas import tpu as pltpu
import functools

HD = 128
BLK = 128
M = 5


loss_scale = 64.0
masked = -1e30


def padded(cells, sides, width):
    for axis, dim in sides:
        count = lax.axis_size(axis)
        ends = count - 1
        head = lax.slice_in_dim(cells, 0, width, axis=dim)
        tail = lax.slice_in_dim(cells, cells.shape[dim] - width, cells.shape[dim], axis=dim)
        cells = jnp.concatenate(
            [
                lax.ppermute(tail, axis, [(i, (i + 1) % count) for i in range(ends)]),
                cells,
                lax.ppermute(head, axis, [((i + 1) % count, i) for i in range(ends)]),
            ],
            axis=dim,
        )
    return cells


def from_behind(value, axis, steps):
    count = lax.axis_size(axis)
    initial, last = (max(0, -steps), min(count, count - steps))
    return lax.ppermute(value, axis, [(source, source + steps) for source in range(initial, last)])


def block_lists(rows, count):
    width = rows.shape[-1]
    running = jnp.cumsum(rows, axis=-1)
    ranks = jnp.arange(1, count + 1, dtype=jnp.int32)
    hits = (rows[..., None, :] == 1) & (running[..., None, :] == ranks[:, None])
    columns = jnp.arange(width, dtype=jnp.int32)
    slot_index = jnp.sum(jnp.where(hits, columns, 0), axis=-1)
    slot_valid = jnp.any(hits, axis=-1)
    return (slot_index, slot_valid)


def attend_rows(query_one, key_window, value_window, slot_index, slot_valid, scale):
    key_tiles = key_window[slot_index]
    value_tiles = value_window[slot_index]
    scores = (
        jnp.einsum("rtd,rmud->rtmu", query_one, key_tiles, preferred_element_type=jnp.float32)
        * scale
    )
    scores = jnp.where(slot_valid[:, None, :, None], scores, masked)
    row_top = jnp.max(scores, axis=(2, 3))
    log_total = row_top + jnp.log(jnp.sum(jnp.exp(scores - row_top[:, :, None, None]), axis=(2, 3)))
    weights = jnp.exp(scores - log_total[:, :, None, None])
    weights_b = weights.astype(jnp.bfloat16)
    attended = jnp.einsum(
        "rtmu,rmud->rtd", weights_b, value_tiles, preferred_element_type=jnp.float32
    )
    grad_out = (loss_scale * attended).astype(jnp.bfloat16)
    row_delta = jnp.sum(grad_out.astype(jnp.float32) * attended, axis=2)
    grad_weights = jnp.einsum(
        "rtd,rmud->rtmu", grad_out, value_tiles, preferred_element_type=jnp.float32
    )
    grad_scores = weights * (grad_weights - row_delta[:, :, None, None])
    grad_scores_b = grad_scores.astype(jnp.bfloat16)
    grad_one = (
        jnp.einsum("rtmu,rmud->rtd", grad_scores_b, key_tiles, preferred_element_type=jnp.float32)
        * scale
    ).astype(jnp.bfloat16)
    return (grad_one, grad_out, log_total, row_delta, weights_b, grad_scores_b)


def one_head(query_one, key_win, value_win, slot_index, slot_valid, scale):
    grad_one, grad_out, log_total, row_delta, weights_b, grad_scores_b = attend_rows(
        query_one, key_win, value_win, slot_index, slot_valid, scale
    )
    value_part = jnp.einsum(
        "rtmu,rtd->rmud", weights_b, grad_out, preferred_element_type=jnp.float32
    )
    key_part = (
        jnp.einsum(
            "rtmu,rtd->rmud", grad_scores_b, query_one, preferred_element_type=jnp.float32
        )
        * scale
    )
    slots = key_win.shape[0]
    picks = (slot_index[:, :, None] == jnp.arange(slots, dtype=slot_index.dtype)) & slot_valid[
        :, :, None
    ]
    picks = picks.astype(jnp.float32)
    key_slots = jnp.einsum("rmw,rmud->wud", picks, key_part, precision=lax.Precision.HIGHEST)
    value_slots = jnp.einsum("rmw,rmud->wud", picks, value_part, precision=lax.Precision.HIGHEST)
    return (grad_one, key_slots, value_slots)


def head_kernel(idx_ref, valid_ref, q_ref, kw_ref, vw_ref, gq_ref, ks_ref, vs_ref, *, scale):
    r = pl.program_id(1)

    @pl.when(r == 0)
    def _():
        ks_ref[...] = jnp.zeros(ks_ref.shape, ks_ref.dtype)
        vs_ref[...] = jnp.zeros(vs_ref.shape, vs_ref.dtype)

    q = q_ref[0, 0]
    slots = [idx_ref[r * M + m] for m in range(M)]
    flags = [valid_ref[r * M + m] > 0 for m in range(M)]
    key_tiles = jnp.concatenate([kw_ref[0, s] for s in slots], axis=0)
    value_tiles = jnp.concatenate([vw_ref[0, s] for s in slots], axis=0)
    nt = (((1,), (1,)), ((), ()))
    tn = (((0,), (0,)), ((), ()))
    column = lax.broadcasted_iota(jnp.int32, (1, M * BLK), 1) // BLK
    usable = column < 0
    for m in range(M):
        usable = usable | ((column == m) & flags[m])
    scores = lax.dot_general(q, key_tiles, nt, preferred_element_type=jnp.float32) * scale
    scores = jnp.where(usable, scores, masked)
    top = scores.max(axis=1, keepdims=True)
    log_total = top + jnp.log(jnp.exp(scores - top).sum(axis=1, keepdims=True))
    weights = jnp.exp(scores - log_total)
    weights_b = weights.astype(jnp.bfloat16)
    attended = jnp.dot(weights_b, value_tiles, preferred_element_type=jnp.float32)
    grad_out = (loss_scale * attended).astype(jnp.bfloat16)
    row_delta = (grad_out.astype(jnp.float32) * attended).sum(axis=1, keepdims=True)
    grad_w = lax.dot_general(grad_out, value_tiles, nt, preferred_element_type=jnp.float32)
    grad_s = (weights * (grad_w - row_delta)).astype(jnp.bfloat16)
    grad_q = jnp.dot(grad_s, key_tiles, preferred_element_type=jnp.float32)
    key_part = lax.dot_general(grad_s, q, tn, preferred_element_type=jnp.float32) * scale
    value_part = lax.dot_general(weights_b, grad_out, tn, preferred_element_type=jnp.float32)
    for m in range(M):
        keep = jnp.where(flags[m], 1.0, 0.0)
        ks_ref[0, slots[m]] = ks_ref[0, slots[m]] + key_part[m * BLK : (m + 1) * BLK] * keep
        vs_ref[0, slots[m]] = vs_ref[0, slots[m]] + value_part[m * BLK : (m + 1) * BLK] * keep
    gq_ref[0, 0] = (grad_q * scale).astype(gq_ref.dtype)


def head_call(query_blocks, key_window, value_window, slot_index, slot_valid, scale):
    heads, rows = query_blocks.shape[:2]
    width = key_window.shape[1]
    idx = slot_index.reshape(-1).astype(jnp.int32)
    val = slot_valid.reshape(-1).astype(jnp.int32)
    whole = lambda h, r, i, v: (h, 0, 0, 0)
    own = lambda h, r, i, v: (h, r, 0, 0)
    spec = pltpu.PrefetchScalarGridSpec(
        num_scalar_prefetch=2,
        grid=(heads, rows),
        in_specs=[
            pl.BlockSpec((1, 1, BLK, HD), own),
            pl.BlockSpec((1, width, BLK, HD), whole),
            pl.BlockSpec((1, width, BLK, HD), whole),
        ],
        out_specs=[
            pl.BlockSpec((1, 1, BLK, HD), own),
            pl.BlockSpec((1, width, BLK, HD), whole),
            pl.BlockSpec((1, width, BLK, HD), whole),
        ],
    )
    return pl.pallas_call(
        functools.partial(head_kernel, scale=scale),
        grid_spec=spec,
        out_shape=[
            jax.ShapeDtypeStruct((heads, rows, BLK, HD), jnp.bfloat16),
            jax.ShapeDtypeStruct((heads, width, BLK, HD), jnp.float32),
            jax.ShapeDtypeStruct((heads, width, BLK, HD), jnp.float32),
        ],
        compiler_params=pltpu.CompilerParams(dimension_semantics=("arbitrary", "arbitrary")),
    )(idx, val, query_blocks, key_window, value_window)


def body(query, keys, values, block_mask):
    scale = HD ** (-0.5)
    tokens_here = query.shape[0]
    heads_all = query.shape[1] // HD
    spread = lax.axis_size("uly")
    heads_here = heads_all // spread
    group_tokens = tokens_here * spread
    group_blocks = group_tokens // BLK
    position = lax.axis_index("blk")
    padded_mask = jnp.pad(block_mask, ((0, 0), (group_blocks, group_blocks)))
    window_mask = lax.dynamic_slice_in_dim(
        padded_mask, position * group_blocks, 3 * group_blocks, 1
    )
    slot_index, slot_valid = block_lists(window_mask, M)

    def heads_major(array):
        split = array.reshape(tokens_here, spread, heads_here, HD)
        return jnp.transpose(split, (2, 1, 0, 3))

    pair = jnp.stack([heads_major(keys), heads_major(values)])
    pair = lax.all_to_all(pair, "uly", split_axis=2, concat_axis=2, tiled=True)
    pair = pair.reshape(2, heads_here, group_tokens, HD)
    beside = padded(pair, (("blk", 2),), group_tokens)
    query_got = lax.all_to_all(heads_major(query), "uly", split_axis=1, concat_axis=1, tiled=True)
    key_window = beside[0].reshape(heads_here, 3 * group_blocks, BLK, HD)
    value_window = beside[1].reshape(heads_here, 3 * group_blocks, BLK, HD)
    query_blocks = query_got.reshape(heads_here, group_blocks, BLK, HD)
    grad_one, key_slots, value_slots = head_call(
        query_blocks, key_window, value_window, slot_index, slot_valid, scale
    )
    slot_sums = jnp.stack([key_slots, value_slots]).reshape(2, heads_here, 3 * group_tokens, HD)
    from_upper = from_behind(
        slot_sums[:, :, :group_tokens].astype(jnp.bfloat16), "blk", -1
    )
    from_lower = from_behind(
        slot_sums[:, :, 2 * group_tokens :].astype(jnp.bfloat16), "blk", 1
    )
    grad_one = grad_one.reshape(heads_here, spread, tokens_here, HD)
    back_query = lax.all_to_all(grad_one, "uly", split_axis=1, concat_axis=1, tiled=True)
    totals = (
        slot_sums[:, :, group_tokens : 2 * group_tokens]
        + from_upper.astype(jnp.float32)
        + from_lower.astype(jnp.float32)
    )
    grads = totals.astype(jnp.bfloat16).reshape(2, heads_here, spread, tokens_here, HD)
    back = lax.all_to_all(grads, "uly", split_axis=2, concat_axis=2, tiled=True)
    back = jnp.concatenate([back_query[None], back])
    back = jnp.transpose(back, (0, 3, 2, 1, 4)).reshape(3, tokens_here, heads_all * HD)
    return (back[0], back[1], back[2])


def solution(mesh):
    in_specs = (
        P(("blk", "uly"), None),
        P(("blk", "uly"), None),
        P(("blk", "uly"), None),
        P("blk", None),
    )
    out_specs = (P(("blk", "uly"), None), P(("blk", "uly"), None), P(("blk", "uly"), None))
    return jax.shard_map(body, mesh=mesh, in_specs=in_specs, out_specs=out_specs, check_vma=False)
```

```python
import jax
import jax.numpy as jnp
from jax import lax
from jax.sharding import PartitionSpec as P
from jax.experimental import pallas as pl
from jax.experimental.pallas import tpu as pltpu
import functools

HD = 128
BLK = 128
M = 5


loss_scale = 64.0
masked = -1e30


def padded(cells, sides, width):
    for axis, dim in sides:
        count = lax.axis_size(axis)
        ends = count - 1
        head = lax.slice_in_dim(cells, 0, width, axis=dim)
        tail = lax.slice_in_dim(cells, cells.shape[dim] - width, cells.shape[dim], axis=dim)
        cells = jnp.concatenate(
            [
                lax.ppermute(tail, axis, [(i, (i + 1) % count) for i in range(ends)]),
                cells,
                lax.ppermute(head, axis, [((i + 1) % count, i) for i in range(ends)]),
            ],
            axis=dim,
        )
    return cells


def from_behind(value, axis, steps):
    count = lax.axis_size(axis)
    initial, last = (max(0, -steps), min(count, count - steps))
    return lax.ppermute(value, axis, [(source, source + steps) for source in range(initial, last)])


def block_lists(rows, count):
    width = rows.shape[-1]
    running = jnp.cumsum(rows, axis=-1)
    ranks = jnp.arange(1, count + 1, dtype=jnp.int32)
    hits = (rows[..., None, :] == 1) & (running[..., None, :] == ranks[:, None])
    columns = jnp.arange(width, dtype=jnp.int32)
    slot_index = jnp.sum(jnp.where(hits, columns, 0), axis=-1)
    slot_valid = jnp.any(hits, axis=-1)
    return (slot_index, slot_valid)


def attend_rows(query_one, key_window, value_window, slot_index, slot_valid, scale):
    key_tiles = key_window[slot_index]
    value_tiles = value_window[slot_index]
    scores = (
        jnp.einsum("rtd,rmud->rtmu", query_one, key_tiles, preferred_element_type=jnp.float32)
        * scale
    )
    scores = jnp.where(slot_valid[:, None, :, None], scores, masked)
    row_top = jnp.max(scores, axis=(2, 3))
    log_total = row_top + jnp.log(jnp.sum(jnp.exp(scores - row_top[:, :, None, None]), axis=(2, 3)))
    weights = jnp.exp(scores - log_total[:, :, None, None])
    weights_b = weights.astype(jnp.bfloat16)
    attended = jnp.einsum(
        "rtmu,rmud->rtd", weights_b, value_tiles, preferred_element_type=jnp.float32
    )
    grad_out = (loss_scale * attended).astype(jnp.bfloat16)
    row_delta = jnp.sum(grad_out.astype(jnp.float32) * attended, axis=2)
    grad_weights = jnp.einsum(
        "rtd,rmud->rtmu", grad_out, value_tiles, preferred_element_type=jnp.float32
    )
    grad_scores = weights * (grad_weights - row_delta[:, :, None, None])
    grad_scores_b = grad_scores.astype(jnp.bfloat16)
    grad_one = (
        jnp.einsum("rtmu,rmud->rtd", grad_scores_b, key_tiles, preferred_element_type=jnp.float32)
        * scale
    ).astype(jnp.bfloat16)
    return (grad_one, grad_out, log_total, row_delta, weights_b, grad_scores_b)


def one_head(query_one, key_win, value_win, slot_index, slot_valid, scale):
    grad_one, grad_out, log_total, row_delta, weights_b, grad_scores_b = attend_rows(
        query_one, key_win, value_win, slot_index, slot_valid, scale
    )
    value_part = jnp.einsum(
        "rtmu,rtd->rmud", weights_b, grad_out, preferred_element_type=jnp.float32
    )
    key_part = (
        jnp.einsum(
            "rtmu,rtd->rmud", grad_scores_b, query_one, preferred_element_type=jnp.float32
        )
        * scale
    )
    slots = key_win.shape[0]
    picks = (slot_index[:, :, None] == jnp.arange(slots, dtype=slot_index.dtype)) & slot_valid[
        :, :, None
    ]
    picks = picks.astype(jnp.float32)
    key_slots = jnp.einsum("rmw,rmud->wud", picks, key_part, precision=lax.Precision.HIGHEST)
    value_slots = jnp.einsum("rmw,rmud->wud", picks, value_part, precision=lax.Precision.HIGHEST)
    return (grad_one, key_slots, value_slots)


def head_kernel(idx_ref, valid_ref, q_ref, kw_ref, vw_ref, gq_ref, ks_ref, vs_ref, *, scale):
    ks_ref[...] = jnp.zeros(ks_ref.shape, ks_ref.dtype)
    vs_ref[...] = jnp.zeros(vs_ref.shape, vs_ref.dtype)
    nt = (((1,), (1,)), ((), ()))
    tn = (((0,), (0,)), ((), ()))
    column = lax.broadcasted_iota(jnp.int32, (1, M * BLK), 1) // BLK

    def step(r, carry):
        q = q_ref[0, r]
        slots = [idx_ref[r * M + m] for m in range(M)]
        flags = [valid_ref[r * M + m] > 0 for m in range(M)]
        key_tiles = jnp.concatenate([kw_ref[0, s] for s in slots], axis=0)
        value_tiles = jnp.concatenate([vw_ref[0, s] for s in slots], axis=0)
        usable = column < 0
        for m in range(M):
            usable = usable | ((column == m) & flags[m])
        scores = lax.dot_general(q, key_tiles, nt, preferred_element_type=jnp.float32) * scale
        scores = jnp.where(usable, scores, masked)
        top = scores.max(axis=1, keepdims=True)
        log_total = top + jnp.log(jnp.exp(scores - top).sum(axis=1, keepdims=True))
        weights = jnp.exp(scores - log_total)
        weights_b = weights.astype(jnp.bfloat16)
        attended = jnp.dot(weights_b, value_tiles, preferred_element_type=jnp.float32)
        grad_out = (loss_scale * attended).astype(jnp.bfloat16)
        row_delta = (grad_out.astype(jnp.float32) * attended).sum(axis=1, keepdims=True)
        grad_w = lax.dot_general(grad_out, value_tiles, nt, preferred_element_type=jnp.float32)
        grad_s = (weights * (grad_w - row_delta)).astype(jnp.bfloat16)
        grad_q = jnp.dot(grad_s, key_tiles, preferred_element_type=jnp.float32)
        key_part = lax.dot_general(grad_s, q, tn, preferred_element_type=jnp.float32) * scale
        value_part = lax.dot_general(weights_b, grad_out, tn, preferred_element_type=jnp.float32)
        for m in range(M):
            keep = jnp.where(flags[m], 1.0, 0.0)
            ks_ref[0, slots[m]] = ks_ref[0, slots[m]] + key_part[m * BLK : (m + 1) * BLK] * keep
            vs_ref[0, slots[m]] = vs_ref[0, slots[m]] + value_part[m * BLK : (m + 1) * BLK] * keep
        gq_ref[0, r] = (grad_q * scale).astype(gq_ref.dtype)
        return carry

    lax.fori_loop(0, q_ref.shape[1], step, 0)


def head_call(query_blocks, key_window, value_window, slot_index, slot_valid, scale):
    heads, rows = query_blocks.shape[:2]
    width = key_window.shape[1]
    idx = slot_index.reshape(-1).astype(jnp.int32)
    val = slot_valid.reshape(-1).astype(jnp.int32)
    whole = lambda h, i, v: (h, 0, 0, 0)
    spec = pltpu.PrefetchScalarGridSpec(
        num_scalar_prefetch=2,
        grid=(heads,),
        in_specs=[
            pl.BlockSpec((1, rows, BLK, HD), whole),
            pl.BlockSpec((1, width, BLK, HD), whole),
            pl.BlockSpec((1, width, BLK, HD), whole),
        ],
        out_specs=[
            pl.BlockSpec((1, rows, BLK, HD), whole),
            pl.BlockSpec((1, width, BLK, HD), whole),
            pl.BlockSpec((1, width, BLK, HD), whole),
        ],
    )
    return pl.pallas_call(
        functools.partial(head_kernel, scale=scale),
        grid_spec=spec,
        out_shape=[
            jax.ShapeDtypeStruct((heads, rows, BLK, HD), jnp.bfloat16),
            jax.ShapeDtypeStruct((heads, width, BLK, HD), jnp.float32),
            jax.ShapeDtypeStruct((heads, width, BLK, HD), jnp.float32),
        ],
        compiler_params=pltpu.CompilerParams(dimension_semantics=("arbitrary",)),
    )(idx, val, query_blocks, key_window, value_window)


def body(query, keys, values, block_mask):
    scale = HD ** (-0.5)
    tokens_here = query.shape[0]
    heads_all = query.shape[1] // HD
    spread = lax.axis_size("uly")
    heads_here = heads_all // spread
    group_tokens = tokens_here * spread
    group_blocks = group_tokens // BLK
    position = lax.axis_index("blk")
    padded_mask = jnp.pad(block_mask, ((0, 0), (group_blocks, group_blocks)))
    window_mask = lax.dynamic_slice_in_dim(
        padded_mask, position * group_blocks, 3 * group_blocks, 1
    )
    slot_index, slot_valid = block_lists(window_mask, M)

    def heads_major(array):
        split = array.reshape(tokens_here, spread, heads_here, HD)
        return jnp.transpose(split, (2, 1, 0, 3))

    pair = jnp.stack([heads_major(keys), heads_major(values)])
    pair = lax.all_to_all(pair, "uly", split_axis=2, concat_axis=2, tiled=True)
    pair = pair.reshape(2, heads_here, group_tokens, HD)
    beside = padded(pair, (("blk", 2),), group_tokens)
    query_got = lax.all_to_all(heads_major(query), "uly", split_axis=1, concat_axis=1, tiled=True)
    key_window = beside[0].reshape(heads_here, 3 * group_blocks, BLK, HD)
    value_window = beside[1].reshape(heads_here, 3 * group_blocks, BLK, HD)
    query_blocks = query_got.reshape(heads_here, group_blocks, BLK, HD)
    grad_one, key_slots, value_slots = head_call(
        query_blocks, key_window, value_window, slot_index, slot_valid, scale
    )
    slot_sums = jnp.stack([key_slots, value_slots]).reshape(2, heads_here, 3 * group_tokens, HD)
    from_upper = from_behind(
        slot_sums[:, :, :group_tokens].astype(jnp.bfloat16), "blk", -1
    )
    from_lower = from_behind(
        slot_sums[:, :, 2 * group_tokens :].astype(jnp.bfloat16), "blk", 1
    )
    grad_one = grad_one.reshape(heads_here, spread, tokens_here, HD)
    back_query = lax.all_to_all(grad_one, "uly", split_axis=1, concat_axis=1, tiled=True)
    totals = (
        slot_sums[:, :, group_tokens : 2 * group_tokens]
        + from_upper.astype(jnp.float32)
        + from_lower.astype(jnp.float32)
    )
    grads = totals.astype(jnp.bfloat16).reshape(2, heads_here, spread, tokens_here, HD)
    back = lax.all_to_all(grads, "uly", split_axis=2, concat_axis=2, tiled=True)
    back = jnp.concatenate([back_query[None], back])
    back = jnp.transpose(back, (0, 3, 2, 1, 4)).reshape(3, tokens_here, heads_all * HD)
    return (back[0], back[1], back[2])


def solution(mesh):
    in_specs = (
        P(("blk", "uly"), None),
        P(("blk", "uly"), None),
        P(("blk", "uly"), None),
        P("blk", None),
    )
    out_specs = (P(("blk", "uly"), None), P(("blk", "uly"), None), P(("blk", "uly"), None))
    return jax.shard_map(body, mesh=mesh, in_specs=in_specs, out_specs=out_specs, check_vma=False)
```

```python
import jax
import jax.numpy as jnp
from jax import lax
from jax.sharding import PartitionSpec as P
from jax.experimental import pallas as pl
from jax.experimental.pallas import tpu as pltpu
import functools

HD = 128
BLK = 128
M = 5


loss_scale = 64.0
masked = -1e30


def padded(cells, sides, width):
    for axis, dim in sides:
        count = lax.axis_size(axis)
        ends = count - 1
        head = lax.slice_in_dim(cells, 0, width, axis=dim)
        tail = lax.slice_in_dim(cells, cells.shape[dim] - width, cells.shape[dim], axis=dim)
        cells = jnp.concatenate(
            [
                lax.ppermute(tail, axis, [(i, (i + 1) % count) for i in range(ends)]),
                cells,
                lax.ppermute(head, axis, [((i + 1) % count, i) for i in range(ends)]),
            ],
            axis=dim,
        )
    return cells


def from_behind(value, axis, steps):
    count = lax.axis_size(axis)
    initial, last = (max(0, -steps), min(count, count - steps))
    return lax.ppermute(value, axis, [(source, source + steps) for source in range(initial, last)])


def block_lists(rows, count):
    width = rows.shape[-1]
    running = jnp.cumsum(rows, axis=-1)
    ranks = jnp.arange(1, count + 1, dtype=jnp.int32)
    hits = (rows[..., None, :] == 1) & (running[..., None, :] == ranks[:, None])
    columns = jnp.arange(width, dtype=jnp.int32)
    slot_index = jnp.sum(jnp.where(hits, columns, 0), axis=-1)
    slot_valid = jnp.any(hits, axis=-1)
    return (slot_index, slot_valid)


def attend_rows(query_one, key_window, value_window, slot_index, slot_valid, scale):
    key_tiles = key_window[slot_index]
    value_tiles = value_window[slot_index]
    scores = (
        jnp.einsum("rtd,rmud->rtmu", query_one, key_tiles, preferred_element_type=jnp.float32)
        * scale
    )
    scores = jnp.where(slot_valid[:, None, :, None], scores, masked)
    row_top = jnp.max(scores, axis=(2, 3))
    log_total = row_top + jnp.log(jnp.sum(jnp.exp(scores - row_top[:, :, None, None]), axis=(2, 3)))
    weights = jnp.exp(scores - log_total[:, :, None, None])
    weights_b = weights.astype(jnp.bfloat16)
    attended = jnp.einsum(
        "rtmu,rmud->rtd", weights_b, value_tiles, preferred_element_type=jnp.float32
    )
    grad_out = (loss_scale * attended).astype(jnp.bfloat16)
    row_delta = jnp.sum(grad_out.astype(jnp.float32) * attended, axis=2)
    grad_weights = jnp.einsum(
        "rtd,rmud->rtmu", grad_out, value_tiles, preferred_element_type=jnp.float32
    )
    grad_scores = weights * (grad_weights - row_delta[:, :, None, None])
    grad_scores_b = grad_scores.astype(jnp.bfloat16)
    grad_one = (
        jnp.einsum("rtmu,rmud->rtd", grad_scores_b, key_tiles, preferred_element_type=jnp.float32)
        * scale
    ).astype(jnp.bfloat16)
    return (grad_one, grad_out, log_total, row_delta, weights_b, grad_scores_b)


def one_head(query_one, key_win, value_win, slot_index, slot_valid, scale):
    grad_one, grad_out, log_total, row_delta, weights_b, grad_scores_b = attend_rows(
        query_one, key_win, value_win, slot_index, slot_valid, scale
    )
    value_part = jnp.einsum(
        "rtmu,rtd->rmud", weights_b, grad_out, preferred_element_type=jnp.float32
    )
    key_part = (
        jnp.einsum(
            "rtmu,rtd->rmud", grad_scores_b, query_one, preferred_element_type=jnp.float32
        )
        * scale
    )
    slots = key_win.shape[0]
    picks = (slot_index[:, :, None] == jnp.arange(slots, dtype=slot_index.dtype)) & slot_valid[
        :, :, None
    ]
    picks = picks.astype(jnp.float32)
    key_slots = jnp.einsum("rmw,rmud->wud", picks, key_part, precision=lax.Precision.HIGHEST)
    value_slots = jnp.einsum("rmw,rmud->wud", picks, value_part, precision=lax.Precision.HIGHEST)
    return (grad_one, key_slots, value_slots)


def head_kernel(
    idx_ref, valid_ref, q_ref, kw_ref, vw_ref, gq_ref, lo_ref, mid_ref, hi_ref, kacc, vacc, *, scale
):
    kacc[...] = jnp.zeros(kacc.shape, kacc.dtype)
    vacc[...] = jnp.zeros(vacc.shape, vacc.dtype)
    nt = (((1,), (1,)), ((), ()))
    tn = (((0,), (0,)), ((), ()))
    column = lax.broadcasted_iota(jnp.int32, (1, M * BLK), 1) // BLK
    rows = q_ref.shape[1]

    def step(r, carry):
        q = q_ref[0, r]
        slots = [idx_ref[r * M + m] for m in range(M)]
        flags = [valid_ref[r * M + m] > 0 for m in range(M)]
        key_tiles = jnp.concatenate([kw_ref[0, 0, s] for s in slots], axis=0)
        value_tiles = jnp.concatenate([vw_ref[0, 0, s] for s in slots], axis=0)
        usable = column < 0
        for m in range(M):
            usable = usable | ((column == m) & flags[m])
        scores = lax.dot_general(q, key_tiles, nt, preferred_element_type=jnp.float32) * scale
        scores = jnp.where(usable, scores, masked)
        top = scores.max(axis=1, keepdims=True)
        log_total = top + jnp.log(jnp.exp(scores - top).sum(axis=1, keepdims=True))
        weights = jnp.exp(scores - log_total)
        weights_b = weights.astype(jnp.bfloat16)
        attended = jnp.dot(weights_b, value_tiles, preferred_element_type=jnp.float32)
        grad_out = (loss_scale * attended).astype(jnp.bfloat16)
        row_delta = (grad_out.astype(jnp.float32) * attended).sum(axis=1, keepdims=True)
        grad_w = lax.dot_general(grad_out, value_tiles, nt, preferred_element_type=jnp.float32)
        grad_s = (weights * (grad_w - row_delta)).astype(jnp.bfloat16)
        grad_q = jnp.dot(grad_s, key_tiles, preferred_element_type=jnp.float32)
        key_part = lax.dot_general(grad_s, q, tn, preferred_element_type=jnp.float32) * scale
        value_part = lax.dot_general(weights_b, grad_out, tn, preferred_element_type=jnp.float32)
        for m in range(M):
            keep = jnp.where(flags[m], 1.0, 0.0)
            kacc[slots[m]] = kacc[slots[m]] + key_part[m * BLK : (m + 1) * BLK] * keep
            vacc[slots[m]] = vacc[slots[m]] + value_part[m * BLK : (m + 1) * BLK] * keep
        gq_ref[0, r] = (grad_q * scale).astype(gq_ref.dtype)
        return carry

    lax.fori_loop(0, rows, step, 0, unroll=True)
    lo_ref[0, 0] = kacc[0:rows].astype(lo_ref.dtype)
    lo_ref[1, 0] = vacc[0:rows].astype(lo_ref.dtype)
    mid_ref[0, 0] = kacc[rows : 2 * rows]
    mid_ref[1, 0] = vacc[rows : 2 * rows]
    hi_ref[0, 0] = kacc[2 * rows : 3 * rows].astype(hi_ref.dtype)
    hi_ref[1, 0] = vacc[2 * rows : 3 * rows].astype(hi_ref.dtype)


def head_call(query_blocks, window, slot_index, slot_valid, scale):
    heads, rows = query_blocks.shape[:2]
    width = window.shape[2]
    idx = slot_index.reshape(-1).astype(jnp.int32)
    val = slot_valid.reshape(-1).astype(jnp.int32)
    own = lambda h, i, v: (h, 0, 0, 0)
    keys_of = lambda h, i, v: (0, h, 0, 0, 0)
    values_of = lambda h, i, v: (1, h, 0, 0, 0)
    edges = pl.BlockSpec((2, 1, rows, BLK, HD), keys_of)
    spec = pltpu.PrefetchScalarGridSpec(
        num_scalar_prefetch=2,
        grid=(heads,),
        in_specs=[
            pl.BlockSpec((1, rows, BLK, HD), own),
            pl.BlockSpec((1, 1, width, BLK, HD), keys_of),
            pl.BlockSpec((1, 1, width, BLK, HD), values_of),
        ],
        out_specs=[pl.BlockSpec((1, rows, BLK, HD), own), edges, edges, edges],
        scratch_shapes=[
            pltpu.VMEM((width, BLK, HD), jnp.float32),
            pltpu.VMEM((width, BLK, HD), jnp.float32),
        ],
    )
    return pl.pallas_call(
        functools.partial(head_kernel, scale=scale),
        grid_spec=spec,
        out_shape=[
            jax.ShapeDtypeStruct((heads, rows, BLK, HD), jnp.bfloat16),
            jax.ShapeDtypeStruct((2, heads, rows, BLK, HD), jnp.bfloat16),
            jax.ShapeDtypeStruct((2, heads, rows, BLK, HD), jnp.float32),
            jax.ShapeDtypeStruct((2, heads, rows, BLK, HD), jnp.bfloat16),
        ],
        compiler_params=pltpu.CompilerParams(dimension_semantics=("arbitrary",)),
    )(idx, val, query_blocks, window, window)


def body(query, keys, values, block_mask):
    scale = HD ** (-0.5)
    tokens_here = query.shape[0]
    heads_all = query.shape[1] // HD
    spread = lax.axis_size("uly")
    heads_here = heads_all // spread
    group_tokens = tokens_here * spread
    group_blocks = group_tokens // BLK
    position = lax.axis_index("blk")
    padded_mask = jnp.pad(block_mask, ((0, 0), (group_blocks, group_blocks)))
    window_mask = lax.dynamic_slice_in_dim(
        padded_mask, position * group_blocks, 3 * group_blocks, 1
    )
    slot_index, slot_valid = block_lists(window_mask, M)

    def heads_major(array):
        split = array.reshape(tokens_here, spread, heads_here, HD)
        return jnp.transpose(split, (2, 1, 0, 3))

    pair = jnp.stack([heads_major(keys), heads_major(values)])
    pair = lax.all_to_all(pair, "uly", split_axis=2, concat_axis=2, tiled=True)
    pair = pair.reshape(2, heads_here, group_tokens, HD)
    beside = padded(pair, (("blk", 2),), group_tokens)
    query_got = lax.all_to_all(heads_major(query), "uly", split_axis=1, concat_axis=1, tiled=True)
    window = beside.reshape(2, heads_here, 3 * group_blocks, BLK, HD)
    query_blocks = query_got.reshape(heads_here, group_blocks, BLK, HD)
    grad_one, lower, middle, upper = head_call(
        query_blocks, window, slot_index, slot_valid, scale
    )
    from_upper = from_behind(lower.reshape(2, heads_here, group_tokens, HD), "blk", -1)
    from_lower = from_behind(upper.reshape(2, heads_here, group_tokens, HD), "blk", 1)
    grad_one = grad_one.reshape(heads_here, spread, tokens_here, HD)
    back_query = lax.all_to_all(grad_one, "uly", split_axis=1, concat_axis=1, tiled=True)
    totals = (
        middle.reshape(2, heads_here, group_tokens, HD)
        + from_upper.astype(jnp.float32)
        + from_lower.astype(jnp.float32)
    )
    grads = totals.astype(jnp.bfloat16).reshape(2, heads_here, spread, tokens_here, HD)
    back = lax.all_to_all(grads, "uly", split_axis=2, concat_axis=2, tiled=True)
    back = jnp.concatenate([back_query[None], back])
    back = jnp.transpose(back, (0, 3, 2, 1, 4)).reshape(3, tokens_here, heads_all * HD)
    return (back[0], back[1], back[2])


def solution(mesh):
    in_specs = (
        P(("blk", "uly"), None),
        P(("blk", "uly"), None),
        P(("blk", "uly"), None),
        P("blk", None),
    )
    out_specs = (P(("blk", "uly"), None), P(("blk", "uly"), None), P(("blk", "uly"), None))
    return jax.shard_map(body, mesh=mesh, in_specs=in_specs, out_specs=out_specs, check_vma=False)
```

```python
import jax
import jax.numpy as jnp
from jax import lax
from jax.sharding import PartitionSpec as P
from jax.experimental import pallas as pl
from jax.experimental.pallas import tpu as pltpu
import functools

HD = 128
BLK = 128
M = 5


loss_scale = 64.0
masked = -1e30


def padded(cells, sides, width):
    for axis, dim in sides:
        count = lax.axis_size(axis)
        ends = count - 1
        head = lax.slice_in_dim(cells, 0, width, axis=dim)
        tail = lax.slice_in_dim(cells, cells.shape[dim] - width, cells.shape[dim], axis=dim)
        cells = jnp.concatenate(
            [
                lax.ppermute(tail, axis, [(i, (i + 1) % count) for i in range(ends)]),
                cells,
                lax.ppermute(head, axis, [((i + 1) % count, i) for i in range(ends)]),
            ],
            axis=dim,
        )
    return cells


def from_behind(value, axis, steps):
    count = lax.axis_size(axis)
    initial, last = (max(0, -steps), min(count, count - steps))
    return lax.ppermute(value, axis, [(source, source + steps) for source in range(initial, last)])


def block_lists(rows, count):
    width = rows.shape[-1]
    running = jnp.cumsum(rows, axis=-1)
    ranks = jnp.arange(1, count + 1, dtype=jnp.int32)
    hits = (rows[..., None, :] == 1) & (running[..., None, :] == ranks[:, None])
    columns = jnp.arange(width, dtype=jnp.int32)
    slot_index = jnp.sum(jnp.where(hits, columns, 0), axis=-1)
    slot_valid = jnp.any(hits, axis=-1)
    return (slot_index, slot_valid)


def attend_rows(query_one, key_window, value_window, slot_index, slot_valid, scale):
    key_tiles = key_window[slot_index]
    value_tiles = value_window[slot_index]
    scores = (
        jnp.einsum("rtd,rmud->rtmu", query_one, key_tiles, preferred_element_type=jnp.float32)
        * scale
    )
    scores = jnp.where(slot_valid[:, None, :, None], scores, masked)
    row_top = jnp.max(scores, axis=(2, 3))
    log_total = row_top + jnp.log(jnp.sum(jnp.exp(scores - row_top[:, :, None, None]), axis=(2, 3)))
    weights = jnp.exp(scores - log_total[:, :, None, None])
    weights_b = weights.astype(jnp.bfloat16)
    attended = jnp.einsum(
        "rtmu,rmud->rtd", weights_b, value_tiles, preferred_element_type=jnp.float32
    )
    grad_out = (loss_scale * attended).astype(jnp.bfloat16)
    row_delta = jnp.sum(grad_out.astype(jnp.float32) * attended, axis=2)
    grad_weights = jnp.einsum(
        "rtd,rmud->rtmu", grad_out, value_tiles, preferred_element_type=jnp.float32
    )
    grad_scores = weights * (grad_weights - row_delta[:, :, None, None])
    grad_scores_b = grad_scores.astype(jnp.bfloat16)
    grad_one = (
        jnp.einsum("rtmu,rmud->rtd", grad_scores_b, key_tiles, preferred_element_type=jnp.float32)
        * scale
    ).astype(jnp.bfloat16)
    return (grad_one, grad_out, log_total, row_delta, weights_b, grad_scores_b)


def one_head(query_one, key_win, value_win, slot_index, slot_valid, scale):
    grad_one, grad_out, log_total, row_delta, weights_b, grad_scores_b = attend_rows(
        query_one, key_win, value_win, slot_index, slot_valid, scale
    )
    value_part = jnp.einsum(
        "rtmu,rtd->rmud", weights_b, grad_out, preferred_element_type=jnp.float32
    )
    key_part = (
        jnp.einsum(
            "rtmu,rtd->rmud", grad_scores_b, query_one, preferred_element_type=jnp.float32
        )
        * scale
    )
    slots = key_win.shape[0]
    picks = (slot_index[:, :, None] == jnp.arange(slots, dtype=slot_index.dtype)) & slot_valid[
        :, :, None
    ]
    picks = picks.astype(jnp.float32)
    key_slots = jnp.einsum("rmw,rmud->wud", picks, key_part, precision=lax.Precision.HIGHEST)
    value_slots = jnp.einsum("rmw,rmud->wud", picks, value_part, precision=lax.Precision.HIGHEST)
    return (grad_one, key_slots, value_slots)


def head_kernel(
    idx_ref, valid_ref, q_ref, kd_ref, vd_ref, ko_ref, vo_ref, ku_ref, vu_ref,
    gq_ref, lo_ref, mid_ref, hi_ref, kacc, vacc, *, scale
):
    kacc[...] = jnp.zeros(kacc.shape, kacc.dtype)
    vacc[...] = jnp.zeros(vacc.shape, vacc.dtype)
    nt = (((1,), (1,)), ((), ()))
    tn = (((0,), (0,)), ((), ()))
    column = lax.broadcasted_iota(jnp.int32, (1, M * BLK), 1) // BLK
    rows = q_ref.shape[1]

    def tile_of(down, here, up, s):
        local = s % rows
        return lax.cond(
            s < rows,
            lambda: down[0, 0, local],
            lambda: lax.cond(s < 2 * rows, lambda: here[0, 0, local], lambda: up[0, 0, local]),
        )

    def step(r, carry):
        q = q_ref[0, r]
        slots = [idx_ref[r * M + m] for m in range(M)]
        flags = [valid_ref[r * M + m] > 0 for m in range(M)]
        key_tiles = jnp.concatenate([tile_of(kd_ref, ko_ref, ku_ref, s) for s in slots], axis=0)
        value_tiles = jnp.concatenate([tile_of(vd_ref, vo_ref, vu_ref, s) for s in slots], axis=0)
        usable = column < 0
        for m in range(M):
            usable = usable | ((column == m) & flags[m])
        scores = lax.dot_general(q, key_tiles, nt, preferred_element_type=jnp.float32) * scale
        scores = jnp.where(usable, scores, masked)
        top = scores.max(axis=1, keepdims=True)
        log_total = top + jnp.log(jnp.exp(scores - top).sum(axis=1, keepdims=True))
        weights = jnp.exp(scores - log_total)
        weights_b = weights.astype(jnp.bfloat16)
        attended = jnp.dot(weights_b, value_tiles, preferred_element_type=jnp.float32)
        grad_out = (loss_scale * attended).astype(jnp.bfloat16)
        row_delta = (grad_out.astype(jnp.float32) * attended).sum(axis=1, keepdims=True)
        grad_w = lax.dot_general(grad_out, value_tiles, nt, preferred_element_type=jnp.float32)
        grad_s = (weights * (grad_w - row_delta)).astype(jnp.bfloat16)
        grad_q = jnp.dot(grad_s, key_tiles, preferred_element_type=jnp.float32)
        key_part = lax.dot_general(grad_s, q, tn, preferred_element_type=jnp.float32) * scale
        value_part = lax.dot_general(weights_b, grad_out, tn, preferred_element_type=jnp.float32)
        for m in range(M):
            keep = jnp.where(flags[m], 1.0, 0.0)
            kacc[slots[m]] = kacc[slots[m]] + key_part[m * BLK : (m + 1) * BLK] * keep
            vacc[slots[m]] = vacc[slots[m]] + value_part[m * BLK : (m + 1) * BLK] * keep
        gq_ref[0, r] = (grad_q * scale).astype(gq_ref.dtype)
        return carry

    lax.fori_loop(0, rows, step, 0, unroll=True)
    lo_ref[0, 0] = kacc[0:rows].astype(lo_ref.dtype)
    lo_ref[1, 0] = vacc[0:rows].astype(lo_ref.dtype)
    mid_ref[0, 0] = kacc[rows : 2 * rows]
    mid_ref[1, 0] = vacc[rows : 2 * rows]
    hi_ref[0, 0] = kacc[2 * rows : 3 * rows].astype(hi_ref.dtype)
    hi_ref[1, 0] = vacc[2 * rows : 3 * rows].astype(hi_ref.dtype)


def head_call(query_blocks, down, here, up, slot_index, slot_valid, scale):
    heads, rows = query_blocks.shape[:2]
    idx = slot_index.reshape(-1).astype(jnp.int32)
    val = slot_valid.reshape(-1).astype(jnp.int32)
    own = lambda h, i, v: (h, 0, 0, 0)
    keys_of = lambda h, i, v: (0, h, 0, 0, 0)
    values_of = lambda h, i, v: (1, h, 0, 0, 0)
    piece = (1, 1, rows, BLK, HD)
    edges = pl.BlockSpec((2, 1, rows, BLK, HD), keys_of)
    spec = pltpu.PrefetchScalarGridSpec(
        num_scalar_prefetch=2,
        grid=(heads,),
        in_specs=[pl.BlockSpec((1, rows, BLK, HD), own)]
        + [pl.BlockSpec(piece, f) for _ in range(3) for f in (keys_of, values_of)],
        out_specs=[pl.BlockSpec((1, rows, BLK, HD), own), edges, edges, edges],
        scratch_shapes=[
            pltpu.VMEM((3 * rows, BLK, HD), jnp.float32),
            pltpu.VMEM((3 * rows, BLK, HD), jnp.float32),
        ],
    )
    return pl.pallas_call(
        functools.partial(head_kernel, scale=scale),
        grid_spec=spec,
        out_shape=[
            jax.ShapeDtypeStruct((heads, rows, BLK, HD), jnp.bfloat16),
            jax.ShapeDtypeStruct((2, heads, rows, BLK, HD), jnp.bfloat16),
            jax.ShapeDtypeStruct((2, heads, rows, BLK, HD), jnp.float32),
            jax.ShapeDtypeStruct((2, heads, rows, BLK, HD), jnp.bfloat16),
        ],
        compiler_params=pltpu.CompilerParams(dimension_semantics=("arbitrary",)),
    )(idx, val, query_blocks, down, down, here, here, up, up)


def body(query, keys, values, block_mask):
    scale = HD ** (-0.5)
    tokens_here = query.shape[0]
    heads_all = query.shape[1] // HD
    spread = lax.axis_size("uly")
    heads_here = heads_all // spread
    group_tokens = tokens_here * spread
    group_blocks = group_tokens // BLK
    position = lax.axis_index("blk")
    padded_mask = jnp.pad(block_mask, ((0, 0), (group_blocks, group_blocks)))
    window_mask = lax.dynamic_slice_in_dim(
        padded_mask, position * group_blocks, 3 * group_blocks, 1
    )
    slot_index, slot_valid = block_lists(window_mask, M)

    def heads_major(array):
        split = array.reshape(tokens_here, spread, heads_here, HD)
        return jnp.transpose(split, (2, 1, 0, 3))

    pair = jnp.stack([heads_major(keys), heads_major(values)])
    pair = lax.all_to_all(pair, "uly", split_axis=2, concat_axis=2, tiled=True)
    pair = pair.reshape(2, heads_here, group_tokens, HD)
    count = lax.axis_size("blk")
    down = lax.ppermute(pair, "blk", [(i, i + 1) for i in range(count - 1)])
    up = lax.ppermute(pair, "blk", [(i + 1, i) for i in range(count - 1)])
    query_got = lax.all_to_all(heads_major(query), "uly", split_axis=1, concat_axis=1, tiled=True)
    shape5 = (2, heads_here, group_blocks, BLK, HD)
    query_blocks = query_got.reshape(heads_here, group_blocks, BLK, HD)
    grad_one, lower, middle, upper = head_call(
        query_blocks,
        down.reshape(shape5),
        pair.reshape(shape5),
        up.reshape(shape5),
        slot_index,
        slot_valid,
        scale,
    )
    from_upper = from_behind(lower.reshape(2, heads_here, group_tokens, HD), "blk", -1)
    from_lower = from_behind(upper.reshape(2, heads_here, group_tokens, HD), "blk", 1)
    grad_one = grad_one.reshape(heads_here, spread, tokens_here, HD)
    back_query = lax.all_to_all(grad_one, "uly", split_axis=1, concat_axis=1, tiled=True)
    totals = (
        middle.reshape(2, heads_here, group_tokens, HD)
        + from_upper.astype(jnp.float32)
        + from_lower.astype(jnp.float32)
    )
    grads = totals.astype(jnp.bfloat16).reshape(2, heads_here, spread, tokens_here, HD)
    back = lax.all_to_all(grads, "uly", split_axis=2, concat_axis=2, tiled=True)
    back_query = jnp.transpose(back_query, (2, 1, 0, 3)).reshape(tokens_here, heads_all * HD)
    back = jnp.transpose(back, (0, 3, 2, 1, 4)).reshape(2, tokens_here, heads_all * HD)
    return (back_query, back[0], back[1])


def solution(mesh):
    in_specs = (
        P(("blk", "uly"), None),
        P(("blk", "uly"), None),
        P(("blk", "uly"), None),
        P("blk", None),
    )
    out_specs = (P(("blk", "uly"), None), P(("blk", "uly"), None), P(("blk", "uly"), None))
    return jax.shard_map(body, mesh=mesh, in_specs=in_specs, out_specs=out_specs, check_vma=False)
```

```python
import jax
import jax.numpy as jnp
from jax import lax
from jax.sharding import PartitionSpec as P
from jax.experimental import pallas as pl
from jax.experimental.pallas import tpu as pltpu
import functools

HD = 128
BLK = 128
M = 5


loss_scale = 64.0
masked = -1e30


def padded(cells, sides, width):
    for axis, dim in sides:
        count = lax.axis_size(axis)
        ends = count - 1
        head = lax.slice_in_dim(cells, 0, width, axis=dim)
        tail = lax.slice_in_dim(cells, cells.shape[dim] - width, cells.shape[dim], axis=dim)
        cells = jnp.concatenate(
            [
                lax.ppermute(tail, axis, [(i, (i + 1) % count) for i in range(ends)]),
                cells,
                lax.ppermute(head, axis, [((i + 1) % count, i) for i in range(ends)]),
            ],
            axis=dim,
        )
    return cells


def from_behind(value, axis, steps):
    count = lax.axis_size(axis)
    initial, last = (max(0, -steps), min(count, count - steps))
    return lax.ppermute(value, axis, [(source, source + steps) for source in range(initial, last)])


def block_lists(rows, count):
    width = rows.shape[-1]
    running = jnp.cumsum(rows, axis=-1)
    ranks = jnp.arange(1, count + 1, dtype=jnp.int32)
    hits = (rows[..., None, :] == 1) & (running[..., None, :] == ranks[:, None])
    columns = jnp.arange(width, dtype=jnp.int32)
    slot_index = jnp.sum(jnp.where(hits, columns, 0), axis=-1)
    slot_valid = jnp.any(hits, axis=-1)
    return (slot_index, slot_valid)


def attend_rows(query_one, key_window, value_window, slot_index, slot_valid, scale):
    key_tiles = key_window[slot_index]
    value_tiles = value_window[slot_index]
    scores = (
        jnp.einsum("rtd,rmud->rtmu", query_one, key_tiles, preferred_element_type=jnp.float32)
        * scale
    )
    scores = jnp.where(slot_valid[:, None, :, None], scores, masked)
    row_top = jnp.max(scores, axis=(2, 3))
    log_total = row_top + jnp.log(jnp.sum(jnp.exp(scores - row_top[:, :, None, None]), axis=(2, 3)))
    weights = jnp.exp(scores - log_total[:, :, None, None])
    weights_b = weights.astype(jnp.bfloat16)
    attended = jnp.einsum(
        "rtmu,rmud->rtd", weights_b, value_tiles, preferred_element_type=jnp.float32
    )
    grad_out = (loss_scale * attended).astype(jnp.bfloat16)
    row_delta = jnp.sum(grad_out.astype(jnp.float32) * attended, axis=2)
    grad_weights = jnp.einsum(
        "rtd,rmud->rtmu", grad_out, value_tiles, preferred_element_type=jnp.float32
    )
    grad_scores = weights * (grad_weights - row_delta[:, :, None, None])
    grad_scores_b = grad_scores.astype(jnp.bfloat16)
    grad_one = (
        jnp.einsum("rtmu,rmud->rtd", grad_scores_b, key_tiles, preferred_element_type=jnp.float32)
        * scale
    ).astype(jnp.bfloat16)
    return (grad_one, grad_out, log_total, row_delta, weights_b, grad_scores_b)


def one_head(query_one, key_win, value_win, slot_index, slot_valid, scale):
    grad_one, grad_out, log_total, row_delta, weights_b, grad_scores_b = attend_rows(
        query_one, key_win, value_win, slot_index, slot_valid, scale
    )
    value_part = jnp.einsum(
        "rtmu,rtd->rmud", weights_b, grad_out, preferred_element_type=jnp.float32
    )
    key_part = (
        jnp.einsum(
            "rtmu,rtd->rmud", grad_scores_b, query_one, preferred_element_type=jnp.float32
        )
        * scale
    )
    slots = key_win.shape[0]
    picks = (slot_index[:, :, None] == jnp.arange(slots, dtype=slot_index.dtype)) & slot_valid[
        :, :, None
    ]
    picks = picks.astype(jnp.float32)
    key_slots = jnp.einsum("rmw,rmud->wud", picks, key_part, precision=lax.Precision.HIGHEST)
    value_slots = jnp.einsum("rmw,rmud->wud", picks, value_part, precision=lax.Precision.HIGHEST)
    return (grad_one, key_slots, value_slots)


def head_kernel(
    idx_ref, valid_ref, q_ref, kw_ref, vw_ref, gq_ref, lo_ref, mid_ref, hi_ref, kacc, vacc, *, scale
):
    kacc[...] = jnp.zeros(kacc.shape, kacc.dtype)
    vacc[...] = jnp.zeros(vacc.shape, vacc.dtype)
    nt = (((1,), (1,)), ((), ()))
    tn = (((0,), (0,)), ((), ()))
    column = lax.broadcasted_iota(jnp.int32, (1, M * BLK), 1) // BLK
    rows = q_ref.shape[1]

    def step(r, carry):
        q = q_ref[0, r]
        slots = [idx_ref[r * M + m] for m in range(M)]
        flags = [valid_ref[r * M + m] > 0 for m in range(M)]
        key_tiles = jnp.concatenate([kw_ref[0, 0, s] for s in slots], axis=0)
        value_tiles = jnp.concatenate([vw_ref[0, 0, s] for s in slots], axis=0)
        usable = column < 0
        for m in range(M):
            usable = usable | ((column == m) & flags[m])
        scores = lax.dot_general(q, key_tiles, nt, preferred_element_type=jnp.float32) * scale
        scores = jnp.where(usable, scores, masked)
        top = scores.max(axis=1, keepdims=True)
        log_total = top + jnp.log(jnp.exp(scores - top).sum(axis=1, keepdims=True))
        weights = jnp.exp(scores - log_total)
        weights_b = weights.astype(jnp.bfloat16)
        attended = jnp.dot(weights_b, value_tiles, preferred_element_type=jnp.float32)
        grad_out = (loss_scale * attended).astype(jnp.bfloat16)
        row_delta = (grad_out.astype(jnp.float32) * attended).sum(axis=1, keepdims=True)
        grad_w = lax.dot_general(grad_out, value_tiles, nt, preferred_element_type=jnp.float32)
        grad_s = (weights * (grad_w - row_delta)).astype(jnp.bfloat16)
        grad_q = jnp.dot(grad_s, key_tiles, preferred_element_type=jnp.float32)
        key_part = lax.dot_general(grad_s, q, tn, preferred_element_type=jnp.float32) * scale
        value_part = lax.dot_general(weights_b, grad_out, tn, preferred_element_type=jnp.float32)
        for m in range(M):
            keep = jnp.where(flags[m], 1.0, 0.0)
            kacc[slots[m]] = kacc[slots[m]] + key_part[m * BLK : (m + 1) * BLK] * keep
            vacc[slots[m]] = vacc[slots[m]] + value_part[m * BLK : (m + 1) * BLK] * keep
        gq_ref[0, r] = (grad_q * scale).astype(gq_ref.dtype)
        return carry

    lax.fori_loop(0, rows, step, 0, unroll=True)
    lo_ref[0, 0] = kacc[0:rows].astype(lo_ref.dtype)
    lo_ref[1, 0] = vacc[0:rows].astype(lo_ref.dtype)
    mid_ref[0, 0] = kacc[rows : 2 * rows]
    mid_ref[1, 0] = vacc[rows : 2 * rows]
    hi_ref[0, 0] = kacc[2 * rows : 3 * rows].astype(hi_ref.dtype)
    hi_ref[1, 0] = vacc[2 * rows : 3 * rows].astype(hi_ref.dtype)


def head_call(query_blocks, window, slot_index, slot_valid, scale):
    heads, rows = query_blocks.shape[:2]
    width = window.shape[2]
    idx = slot_index.reshape(-1).astype(jnp.int32)
    val = slot_valid.reshape(-1).astype(jnp.int32)
    own = lambda h, i, v: (h, 0, 0, 0)
    keys_of = lambda h, i, v: (0, h, 0, 0, 0)
    values_of = lambda h, i, v: (1, h, 0, 0, 0)
    edges = pl.BlockSpec((2, 1, rows, BLK, HD), keys_of)
    spec = pltpu.PrefetchScalarGridSpec(
        num_scalar_prefetch=2,
        grid=(heads,),
        in_specs=[
            pl.BlockSpec((1, rows, BLK, HD), own),
            pl.BlockSpec((1, 1, width, BLK, HD), keys_of),
            pl.BlockSpec((1, 1, width, BLK, HD), values_of),
        ],
        out_specs=[pl.BlockSpec((1, rows, BLK, HD), own), edges, edges, edges],
        scratch_shapes=[
            pltpu.VMEM((width, BLK, HD), jnp.float32),
            pltpu.VMEM((width, BLK, HD), jnp.float32),
        ],
    )
    return pl.pallas_call(
        functools.partial(head_kernel, scale=scale),
        grid_spec=spec,
        out_shape=[
            jax.ShapeDtypeStruct((heads, rows, BLK, HD), jnp.bfloat16),
            jax.ShapeDtypeStruct((2, heads, rows, BLK, HD), jnp.bfloat16),
            jax.ShapeDtypeStruct((2, heads, rows, BLK, HD), jnp.float32),
            jax.ShapeDtypeStruct((2, heads, rows, BLK, HD), jnp.bfloat16),
        ],
        compiler_params=pltpu.CompilerParams(dimension_semantics=("arbitrary",)),
    )(idx, val, query_blocks, window, window)


def body(query, keys, values, block_mask):
    scale = HD ** (-0.5)
    tokens_here = query.shape[0]
    heads_all = query.shape[1] // HD
    spread = lax.axis_size("uly")
    heads_here = heads_all // spread
    group_tokens = tokens_here * spread
    group_blocks = group_tokens // BLK
    position = lax.axis_index("blk")
    padded_mask = jnp.pad(block_mask, ((0, 0), (group_blocks, group_blocks)))
    window_mask = lax.dynamic_slice_in_dim(
        padded_mask, position * group_blocks, 3 * group_blocks, 1
    )
    slot_index, slot_valid = block_lists(window_mask, M)

    def heads_major(array):
        split = array.reshape(tokens_here, spread, heads_here, HD)
        return jnp.transpose(split, (2, 1, 0, 3))

    pair = jnp.stack([heads_major(keys), heads_major(values)])
    pair = lax.all_to_all(pair, "uly", split_axis=2, concat_axis=2, tiled=True)
    pair = pair.reshape(2, heads_here, group_tokens, HD)
    beside = padded(pair, (("blk", 2),), group_tokens)
    query_got = lax.all_to_all(heads_major(query), "uly", split_axis=1, concat_axis=1, tiled=True)
    window = beside.reshape(2, heads_here, 3 * group_blocks, BLK, HD)
    query_blocks = query_got.reshape(heads_here, group_blocks, BLK, HD)
    grad_one, lower, middle, upper = head_call(
        query_blocks, window, slot_index, slot_valid, scale
    )
    from_upper = from_behind(lower.reshape(2, heads_here, group_tokens, HD), "blk", -1)
    from_lower = from_behind(upper.reshape(2, heads_here, group_tokens, HD), "blk", 1)
    grad_one = grad_one.reshape(heads_here, spread, tokens_here, HD)
    back_query = lax.all_to_all(grad_one, "uly", split_axis=1, concat_axis=1, tiled=True)
    totals = (
        middle.reshape(2, heads_here, group_tokens, HD)
        + from_upper.astype(jnp.float32)
        + from_lower.astype(jnp.float32)
    )
    grads = totals.astype(jnp.bfloat16).reshape(2, heads_here, spread, tokens_here, HD)
    back = lax.all_to_all(grads, "uly", split_axis=2, concat_axis=2, tiled=True)
    back_query = jnp.transpose(back_query, (2, 1, 0, 3)).reshape(tokens_here, heads_all * HD)
    back = jnp.transpose(back, (0, 3, 2, 1, 4)).reshape(2, tokens_here, heads_all * HD)
    return (back_query, back[0], back[1])


def solution(mesh):
    in_specs = (
        P(("blk", "uly"), None),
        P(("blk", "uly"), None),
        P(("blk", "uly"), None),
        P("blk", None),
    )
    out_specs = (P(("blk", "uly"), None), P(("blk", "uly"), None), P(("blk", "uly"), None))
    return jax.shard_map(body, mesh=mesh, in_specs=in_specs, out_specs=out_specs, check_vma=False)
```

```python
import jax
import jax.numpy as jnp
from jax import lax
from jax.sharding import PartitionSpec as P
from jax.experimental import pallas as pl
from jax.experimental.pallas import tpu as pltpu
import functools

HD = 128
BLK = 128
M = 5


loss_scale = 64.0
masked = -1e30


def padded(cells, sides, width):
    for axis, dim in sides:
        count = lax.axis_size(axis)
        ends = count - 1
        head = lax.slice_in_dim(cells, 0, width, axis=dim)
        tail = lax.slice_in_dim(cells, cells.shape[dim] - width, cells.shape[dim], axis=dim)
        cells = jnp.concatenate(
            [
                lax.ppermute(tail, axis, [(i, (i + 1) % count) for i in range(ends)]),
                cells,
                lax.ppermute(head, axis, [((i + 1) % count, i) for i in range(ends)]),
            ],
            axis=dim,
        )
    return cells


def from_behind(value, axis, steps):
    count = lax.axis_size(axis)
    initial, last = (max(0, -steps), min(count, count - steps))
    return lax.ppermute(value, axis, [(source, source + steps) for source in range(initial, last)])


def block_lists(rows, count):
    width = rows.shape[-1]
    running = jnp.cumsum(rows, axis=-1)
    ranks = jnp.arange(1, count + 1, dtype=jnp.int32)
    hits = (rows[..., None, :] == 1) & (running[..., None, :] == ranks[:, None])
    columns = jnp.arange(width, dtype=jnp.int32)
    slot_index = jnp.sum(jnp.where(hits, columns, 0), axis=-1)
    slot_valid = jnp.any(hits, axis=-1)
    return (slot_index, slot_valid)


def attend_rows(query_one, key_window, value_window, slot_index, slot_valid, scale):
    key_tiles = key_window[slot_index]
    value_tiles = value_window[slot_index]
    scores = (
        jnp.einsum("rtd,rmud->rtmu", query_one, key_tiles, preferred_element_type=jnp.float32)
        * scale
    )
    scores = jnp.where(slot_valid[:, None, :, None], scores, masked)
    row_top = jnp.max(scores, axis=(2, 3))
    log_total = row_top + jnp.log(jnp.sum(jnp.exp(scores - row_top[:, :, None, None]), axis=(2, 3)))
    weights = jnp.exp(scores - log_total[:, :, None, None])
    weights_b = weights.astype(jnp.bfloat16)
    attended = jnp.einsum(
        "rtmu,rmud->rtd", weights_b, value_tiles, preferred_element_type=jnp.float32
    )
    grad_out = (loss_scale * attended).astype(jnp.bfloat16)
    row_delta = jnp.sum(grad_out.astype(jnp.float32) * attended, axis=2)
    grad_weights = jnp.einsum(
        "rtd,rmud->rtmu", grad_out, value_tiles, preferred_element_type=jnp.float32
    )
    grad_scores = weights * (grad_weights - row_delta[:, :, None, None])
    grad_scores_b = grad_scores.astype(jnp.bfloat16)
    grad_one = (
        jnp.einsum("rtmu,rmud->rtd", grad_scores_b, key_tiles, preferred_element_type=jnp.float32)
        * scale
    ).astype(jnp.bfloat16)
    return (grad_one, grad_out, log_total, row_delta, weights_b, grad_scores_b)


def one_head(query_one, key_win, value_win, slot_index, slot_valid, scale):
    grad_one, grad_out, log_total, row_delta, weights_b, grad_scores_b = attend_rows(
        query_one, key_win, value_win, slot_index, slot_valid, scale
    )
    value_part = jnp.einsum(
        "rtmu,rtd->rmud", weights_b, grad_out, preferred_element_type=jnp.float32
    )
    key_part = (
        jnp.einsum(
            "rtmu,rtd->rmud", grad_scores_b, query_one, preferred_element_type=jnp.float32
        )
        * scale
    )
    slots = key_win.shape[0]
    picks = (slot_index[:, :, None] == jnp.arange(slots, dtype=slot_index.dtype)) & slot_valid[
        :, :, None
    ]
    picks = picks.astype(jnp.float32)
    key_slots = jnp.einsum("rmw,rmud->wud", picks, key_part, precision=lax.Precision.HIGHEST)
    value_slots = jnp.einsum("rmw,rmud->wud", picks, value_part, precision=lax.Precision.HIGHEST)
    return (grad_one, key_slots, value_slots)


def head_kernel(
    idx_ref, valid_ref, q_ref, kw_ref, vw_ref, gq_ref, lo_ref, mid_ref, hi_ref, kacc, vacc, *, scale
):
    kacc[...] = jnp.zeros(kacc.shape, kacc.dtype)
    vacc[...] = jnp.zeros(vacc.shape, vacc.dtype)
    nt = (((1,), (1,)), ((), ()))
    tn = (((0,), (0,)), ((), ()))
    column = lax.broadcasted_iota(jnp.int32, (1, M * BLK), 1) // BLK
    rows = q_ref.shape[1]

    def step(r, carry):
        q = q_ref[0, r]
        slots = [idx_ref[r * M + m] for m in range(M)]
        flags = [valid_ref[r * M + m] > 0 for m in range(M)]
        key_tiles = jnp.concatenate([kw_ref[0, 0, s] for s in slots], axis=0)
        value_tiles = jnp.concatenate([vw_ref[0, 0, s] for s in slots], axis=0)
        usable = column < 0
        for m in range(M):
            usable = usable | ((column == m) & flags[m])
        scores = lax.dot_general(q, key_tiles, nt, preferred_element_type=jnp.float32) * scale
        scores = jnp.where(usable, scores, masked)
        top = scores.max(axis=1, keepdims=True)
        raised = jnp.exp(scores - top)
        weights = raised * (1.0 / raised.sum(axis=1, keepdims=True))
        weights_b = weights.astype(jnp.bfloat16)
        attended = jnp.dot(weights_b, value_tiles, preferred_element_type=jnp.float32)
        grad_out = (loss_scale * attended).astype(jnp.bfloat16)
        row_delta = (grad_out.astype(jnp.float32) * attended).sum(axis=1, keepdims=True)
        grad_w = lax.dot_general(grad_out, value_tiles, nt, preferred_element_type=jnp.float32)
        grad_s = (weights * (grad_w - row_delta)).astype(jnp.bfloat16)
        grad_q = jnp.dot(grad_s, key_tiles, preferred_element_type=jnp.float32)
        key_part = lax.dot_general(grad_s, q, tn, preferred_element_type=jnp.float32) * scale
        value_part = lax.dot_general(weights_b, grad_out, tn, preferred_element_type=jnp.float32)
        for m in range(M):
            keep = jnp.where(flags[m], 1.0, 0.0)
            kacc[slots[m]] = kacc[slots[m]] + key_part[m * BLK : (m + 1) * BLK] * keep
            vacc[slots[m]] = vacc[slots[m]] + value_part[m * BLK : (m + 1) * BLK] * keep
        gq_ref[0, r] = (grad_q * scale).astype(gq_ref.dtype)
        return carry

    lax.fori_loop(0, rows, step, 0, unroll=True)
    lo_ref[0, 0] = kacc[0:rows].astype(lo_ref.dtype)
    lo_ref[1, 0] = vacc[0:rows].astype(lo_ref.dtype)
    mid_ref[0, 0] = kacc[rows : 2 * rows]
    mid_ref[1, 0] = vacc[rows : 2 * rows]
    hi_ref[0, 0] = kacc[2 * rows : 3 * rows].astype(hi_ref.dtype)
    hi_ref[1, 0] = vacc[2 * rows : 3 * rows].astype(hi_ref.dtype)


def head_call(query_blocks, window, slot_index, slot_valid, scale):
    heads, rows = query_blocks.shape[:2]
    width = window.shape[2]
    idx = slot_index.reshape(-1).astype(jnp.int32)
    val = slot_valid.reshape(-1).astype(jnp.int32)
    own = lambda h, i, v: (h, 0, 0, 0)
    keys_of = lambda h, i, v: (0, h, 0, 0, 0)
    values_of = lambda h, i, v: (1, h, 0, 0, 0)
    edges = pl.BlockSpec((2, 1, rows, BLK, HD), keys_of)
    spec = pltpu.PrefetchScalarGridSpec(
        num_scalar_prefetch=2,
        grid=(heads,),
        in_specs=[
            pl.BlockSpec((1, rows, BLK, HD), own),
            pl.BlockSpec((1, 1, width, BLK, HD), keys_of),
            pl.BlockSpec((1, 1, width, BLK, HD), values_of),
        ],
        out_specs=[pl.BlockSpec((1, rows, BLK, HD), own), edges, edges, edges],
        scratch_shapes=[
            pltpu.VMEM((width, BLK, HD), jnp.float32),
            pltpu.VMEM((width, BLK, HD), jnp.float32),
        ],
    )
    return pl.pallas_call(
        functools.partial(head_kernel, scale=scale),
        grid_spec=spec,
        out_shape=[
            jax.ShapeDtypeStruct((heads, rows, BLK, HD), jnp.bfloat16),
            jax.ShapeDtypeStruct((2, heads, rows, BLK, HD), jnp.bfloat16),
            jax.ShapeDtypeStruct((2, heads, rows, BLK, HD), jnp.float32),
            jax.ShapeDtypeStruct((2, heads, rows, BLK, HD), jnp.bfloat16),
        ],
        compiler_params=pltpu.CompilerParams(dimension_semantics=("arbitrary",)),
    )(idx, val, query_blocks, window, window)


def body(query, keys, values, block_mask):
    scale = HD ** (-0.5)
    tokens_here = query.shape[0]
    heads_all = query.shape[1] // HD
    spread = lax.axis_size("uly")
    heads_here = heads_all // spread
    group_tokens = tokens_here * spread
    group_blocks = group_tokens // BLK
    position = lax.axis_index("blk")
    padded_mask = jnp.pad(block_mask, ((0, 0), (group_blocks, group_blocks)))
    window_mask = lax.dynamic_slice_in_dim(
        padded_mask, position * group_blocks, 3 * group_blocks, 1
    )
    slot_index, slot_valid = block_lists(window_mask, M)

    def heads_major(array):
        split = array.reshape(tokens_here, spread, heads_here, HD)
        return jnp.transpose(split, (2, 1, 0, 3))

    pair = jnp.stack([heads_major(keys), heads_major(values)])
    pair = lax.all_to_all(pair, "uly", split_axis=2, concat_axis=2, tiled=True)
    pair = pair.reshape(2, heads_here, group_tokens, HD)
    beside = padded(pair, (("blk", 2),), group_tokens)
    query_got = lax.all_to_all(heads_major(query), "uly", split_axis=1, concat_axis=1, tiled=True)
    window = beside.reshape(2, heads_here, 3 * group_blocks, BLK, HD)
    query_blocks = query_got.reshape(heads_here, group_blocks, BLK, HD)
    grad_one, lower, middle, upper = head_call(
        query_blocks, window, slot_index, slot_valid, scale
    )
    from_upper = from_behind(lower.reshape(2, heads_here, group_tokens, HD), "blk", -1)
    from_lower = from_behind(upper.reshape(2, heads_here, group_tokens, HD), "blk", 1)
    grad_one = grad_one.reshape(heads_here, spread, tokens_here, HD)
    back_query = lax.all_to_all(grad_one, "uly", split_axis=1, concat_axis=1, tiled=True)
    totals = (
        middle.reshape(2, heads_here, group_tokens, HD)
        + from_upper.astype(jnp.float32)
        + from_lower.astype(jnp.float32)
    )
    grads = totals.astype(jnp.bfloat16).reshape(2, heads_here, spread, tokens_here, HD)
    back = lax.all_to_all(grads, "uly", split_axis=2, concat_axis=2, tiled=True)
    back_query = jnp.transpose(back_query, (2, 1, 0, 3)).reshape(tokens_here, heads_all * HD)
    back = jnp.transpose(back, (0, 3, 2, 1, 4)).reshape(2, tokens_here, heads_all * HD)
    return (back_query, back[0], back[1])


def solution(mesh):
    in_specs = (
        P(("blk", "uly"), None),
        P(("blk", "uly"), None),
        P(("blk", "uly"), None),
        P("blk", None),
    )
    out_specs = (P(("blk", "uly"), None), P(("blk", "uly"), None), P(("blk", "uly"), None))
    return jax.shard_map(body, mesh=mesh, in_specs=in_specs, out_specs=out_specs, check_vma=False)
```

```python
import jax
import jax.numpy as jnp
from jax import lax
from jax.sharding import PartitionSpec as P
from jax.experimental import pallas as pl
from jax.experimental.pallas import tpu as pltpu
import functools

HD = 128
BLK = 128
M = 5


loss_scale = 64.0
masked = -1e30


def padded(cells, sides, width):
    for axis, dim in sides:
        count = lax.axis_size(axis)
        ends = count - 1
        head = lax.slice_in_dim(cells, 0, width, axis=dim)
        tail = lax.slice_in_dim(cells, cells.shape[dim] - width, cells.shape[dim], axis=dim)
        cells = jnp.concatenate(
            [
                lax.ppermute(tail, axis, [(i, (i + 1) % count) for i in range(ends)]),
                cells,
                lax.ppermute(head, axis, [((i + 1) % count, i) for i in range(ends)]),
            ],
            axis=dim,
        )
    return cells


def from_behind(value, axis, steps):
    count = lax.axis_size(axis)
    initial, last = (max(0, -steps), min(count, count - steps))
    return lax.ppermute(value, axis, [(source, source + steps) for source in range(initial, last)])


def block_lists(rows, count):
    width = rows.shape[-1]
    running = jnp.cumsum(rows, axis=-1)
    ranks = jnp.arange(1, count + 1, dtype=jnp.int32)
    hits = (rows[..., None, :] == 1) & (running[..., None, :] == ranks[:, None])
    columns = jnp.arange(width, dtype=jnp.int32)
    slot_index = jnp.sum(jnp.where(hits, columns, 0), axis=-1)
    slot_valid = jnp.any(hits, axis=-1)
    return (slot_index, slot_valid)


def attend_rows(query_one, key_window, value_window, slot_index, slot_valid, scale):
    key_tiles = key_window[slot_index]
    value_tiles = value_window[slot_index]
    scores = (
        jnp.einsum("rtd,rmud->rtmu", query_one, key_tiles, preferred_element_type=jnp.float32)
        * scale
    )
    scores = jnp.where(slot_valid[:, None, :, None], scores, masked)
    row_top = jnp.max(scores, axis=(2, 3))
    log_total = row_top + jnp.log(jnp.sum(jnp.exp(scores - row_top[:, :, None, None]), axis=(2, 3)))
    weights = jnp.exp(scores - log_total[:, :, None, None])
    weights_b = weights.astype(jnp.bfloat16)
    attended = jnp.einsum(
        "rtmu,rmud->rtd", weights_b, value_tiles, preferred_element_type=jnp.float32
    )
    grad_out = (loss_scale * attended).astype(jnp.bfloat16)
    row_delta = jnp.sum(grad_out.astype(jnp.float32) * attended, axis=2)
    grad_weights = jnp.einsum(
        "rtd,rmud->rtmu", grad_out, value_tiles, preferred_element_type=jnp.float32
    )
    grad_scores = weights * (grad_weights - row_delta[:, :, None, None])
    grad_scores_b = grad_scores.astype(jnp.bfloat16)
    grad_one = (
        jnp.einsum("rtmu,rmud->rtd", grad_scores_b, key_tiles, preferred_element_type=jnp.float32)
        * scale
    ).astype(jnp.bfloat16)
    return (grad_one, grad_out, log_total, row_delta, weights_b, grad_scores_b)


def one_head(query_one, key_win, value_win, slot_index, slot_valid, scale):
    grad_one, grad_out, log_total, row_delta, weights_b, grad_scores_b = attend_rows(
        query_one, key_win, value_win, slot_index, slot_valid, scale
    )
    value_part = jnp.einsum(
        "rtmu,rtd->rmud", weights_b, grad_out, preferred_element_type=jnp.float32
    )
    key_part = (
        jnp.einsum(
            "rtmu,rtd->rmud", grad_scores_b, query_one, preferred_element_type=jnp.float32
        )
        * scale
    )
    slots = key_win.shape[0]
    picks = (slot_index[:, :, None] == jnp.arange(slots, dtype=slot_index.dtype)) & slot_valid[
        :, :, None
    ]
    picks = picks.astype(jnp.float32)
    key_slots = jnp.einsum("rmw,rmud->wud", picks, key_part, precision=lax.Precision.HIGHEST)
    value_slots = jnp.einsum("rmw,rmud->wud", picks, value_part, precision=lax.Precision.HIGHEST)
    return (grad_one, key_slots, value_slots)


def head_kernel(
    idx_ref, valid_ref, q_ref, kw_ref, vw_ref, gq_ref, lo_ref, mid_ref, hi_ref, kacc, vacc, *, scale
):
    kacc[...] = jnp.zeros(kacc.shape, kacc.dtype)
    vacc[...] = jnp.zeros(vacc.shape, vacc.dtype)
    nt = (((1,), (1,)), ((), ()))
    tn = (((0,), (0,)), ((), ()))
    column = lax.broadcasted_iota(jnp.int32, (1, M * BLK), 1) // BLK
    rows = q_ref.shape[1]

    def step(r, carry):
        q = q_ref[0, r]
        slots = [idx_ref[r * M + m] for m in range(M)]
        flags = [valid_ref[r * M + m] > 0 for m in range(M)]
        key_tiles = jnp.concatenate([kw_ref[0, 0, s] for s in slots], axis=0)
        value_tiles = jnp.concatenate([vw_ref[0, 0, s] for s in slots], axis=0)
        usable = column < 0
        for m in range(M):
            usable = usable | ((column == m) & flags[m])
        scores = lax.dot_general(q, key_tiles, nt, preferred_element_type=jnp.float32) * scale
        scores = jnp.where(usable, scores, masked)
        top = scores.max(axis=1, keepdims=True)
        log_total = top + jnp.log(jnp.exp(scores - top).sum(axis=1, keepdims=True))
        weights = jnp.exp(scores - log_total)
        weights_b = weights.astype(jnp.bfloat16)
        attended = jnp.dot(weights_b, value_tiles, preferred_element_type=jnp.float32)
        grad_out = (loss_scale * attended).astype(jnp.bfloat16)
        row_delta = (grad_out.astype(jnp.float32) * attended).sum(axis=1, keepdims=True)
        grad_w = lax.dot_general(grad_out, value_tiles, nt, preferred_element_type=jnp.float32)
        grad_s = (weights * (grad_w - row_delta)).astype(jnp.bfloat16)
        grad_q = jnp.dot(grad_s, key_tiles, preferred_element_type=jnp.float32)
        key_part = lax.dot_general(grad_s, q, tn, preferred_element_type=jnp.float32) * scale
        value_part = lax.dot_general(weights_b, grad_out, tn, preferred_element_type=jnp.float32)
        for m in range(M):
            keep = jnp.where(flags[m], 1.0, 0.0)
            kacc[slots[m]] = kacc[slots[m]] + key_part[m * BLK : (m + 1) * BLK] * keep
            vacc[slots[m]] = vacc[slots[m]] + value_part[m * BLK : (m + 1) * BLK] * keep
        gq_ref[0, r] = (grad_q * scale).astype(gq_ref.dtype)
        return carry

    lax.fori_loop(0, rows, step, 0, unroll=True)
    lo_ref[0, 0] = kacc[0:rows].astype(lo_ref.dtype)
    lo_ref[1, 0] = vacc[0:rows].astype(lo_ref.dtype)
    mid_ref[0, 0] = kacc[rows : 2 * rows]
    mid_ref[1, 0] = vacc[rows : 2 * rows]
    hi_ref[0, 0] = kacc[2 * rows : 3 * rows].astype(hi_ref.dtype)
    hi_ref[1, 0] = vacc[2 * rows : 3 * rows].astype(hi_ref.dtype)


def head_call(query_blocks, window, slot_index, slot_valid, scale):
    heads, rows = query_blocks.shape[:2]
    width = window.shape[2]
    idx = slot_index.reshape(-1).astype(jnp.int32)
    val = slot_valid.reshape(-1).astype(jnp.int32)
    own = lambda h, i, v: (h, 0, 0, 0)
    keys_of = lambda h, i, v: (0, h, 0, 0, 0)
    values_of = lambda h, i, v: (1, h, 0, 0, 0)
    edges = pl.BlockSpec((2, 1, rows, BLK, HD), keys_of)
    spec = pltpu.PrefetchScalarGridSpec(
        num_scalar_prefetch=2,
        grid=(heads,),
        in_specs=[
            pl.BlockSpec((1, rows, BLK, HD), own),
            pl.BlockSpec((1, 1, width, BLK, HD), keys_of),
            pl.BlockSpec((1, 1, width, BLK, HD), values_of),
        ],
        out_specs=[pl.BlockSpec((1, rows, BLK, HD), own), edges, edges, edges],
        scratch_shapes=[
            pltpu.VMEM((width, BLK, HD), jnp.float32),
            pltpu.VMEM((width, BLK, HD), jnp.float32),
        ],
    )
    return pl.pallas_call(
        functools.partial(head_kernel, scale=scale),
        grid_spec=spec,
        out_shape=[
            jax.ShapeDtypeStruct((heads, rows, BLK, HD), jnp.bfloat16),
            jax.ShapeDtypeStruct((2, heads, rows, BLK, HD), jnp.bfloat16),
            jax.ShapeDtypeStruct((2, heads, rows, BLK, HD), jnp.float32),
            jax.ShapeDtypeStruct((2, heads, rows, BLK, HD), jnp.bfloat16),
        ],
        compiler_params=pltpu.CompilerParams(dimension_semantics=("arbitrary",)),
    )(idx, val, query_blocks, window, window)


def body(query, keys, values, block_mask):
    scale = HD ** (-0.5)
    tokens_here = query.shape[0]
    heads_all = query.shape[1] // HD
    spread = lax.axis_size("uly")
    heads_here = heads_all // spread
    group_tokens = tokens_here * spread
    group_blocks = group_tokens // BLK
    position = lax.axis_index("blk")
    padded_mask = jnp.pad(block_mask, ((0, 0), (group_blocks, group_blocks)))
    window_mask = lax.dynamic_slice_in_dim(
        padded_mask, position * group_blocks, 3 * group_blocks, 1
    )
    slot_index, slot_valid = block_lists(window_mask, M)

    def heads_major(array):
        split = array.reshape(tokens_here, spread, heads_here, HD)
        return jnp.transpose(split, (2, 1, 0, 3))

    pair = jnp.stack([heads_major(keys), heads_major(values)])
    query_sent = heads_major(query)
    pair, query_sent = lax.optimization_barrier((pair, query_sent))
    pair = lax.all_to_all(pair, "uly", split_axis=2, concat_axis=2, tiled=True)
    pair = pair.reshape(2, heads_here, group_tokens, HD)
    beside = padded(pair, (("blk", 2),), group_tokens)
    query_got = lax.all_to_all(query_sent, "uly", split_axis=1, concat_axis=1, tiled=True)
    window = beside.reshape(2, heads_here, 3 * group_blocks, BLK, HD)
    query_blocks = query_got.reshape(heads_here, group_blocks, BLK, HD)
    grad_one, lower, middle, upper = head_call(
        query_blocks, window, slot_index, slot_valid, scale
    )
    from_upper = from_behind(lower.reshape(2, heads_here, group_tokens, HD), "blk", -1)
    from_lower = from_behind(upper.reshape(2, heads_here, group_tokens, HD), "blk", 1)
    grad_one = grad_one.reshape(heads_here, spread, tokens_here, HD)
    back_query = lax.all_to_all(grad_one, "uly", split_axis=1, concat_axis=1, tiled=True)
    totals = (
        middle.reshape(2, heads_here, group_tokens, HD)
        + from_upper.astype(jnp.float32)
        + from_lower.astype(jnp.float32)
    )
    grads = totals.astype(jnp.bfloat16).reshape(2, heads_here, spread, tokens_here, HD)
    back = lax.all_to_all(grads, "uly", split_axis=2, concat_axis=2, tiled=True)
    back_query = jnp.transpose(back_query, (2, 1, 0, 3)).reshape(tokens_here, heads_all * HD)
    back = jnp.transpose(back, (0, 3, 2, 1, 4)).reshape(2, tokens_here, heads_all * HD)
    return (back_query, back[0], back[1])


def solution(mesh):
    in_specs = (
        P(("blk", "uly"), None),
        P(("blk", "uly"), None),
        P(("blk", "uly"), None),
        P("blk", None),
    )
    out_specs = (P(("blk", "uly"), None), P(("blk", "uly"), None), P(("blk", "uly"), None))
    return jax.shard_map(body, mesh=mesh, in_specs=in_specs, out_specs=out_specs, check_vma=False)
```

```python
import jax
import jax.numpy as jnp
from jax import lax
from jax.sharding import PartitionSpec as P
from jax.experimental import pallas as pl
from jax.experimental.pallas import tpu as pltpu
import functools

HD = 128
BLK = 128
M = 5


loss_scale = 64.0
masked = -1e30


def padded(cells, sides, width):
    for axis, dim in sides:
        count = lax.axis_size(axis)
        ends = count - 1
        head = lax.slice_in_dim(cells, 0, width, axis=dim)
        tail = lax.slice_in_dim(cells, cells.shape[dim] - width, cells.shape[dim], axis=dim)
        cells = jnp.concatenate(
            [
                lax.ppermute(tail, axis, [(i, (i + 1) % count) for i in range(ends)]),
                cells,
                lax.ppermute(head, axis, [((i + 1) % count, i) for i in range(ends)]),
            ],
            axis=dim,
        )
    return cells


def from_behind(value, axis, steps):
    count = lax.axis_size(axis)
    initial, last = (max(0, -steps), min(count, count - steps))
    return lax.ppermute(value, axis, [(source, source + steps) for source in range(initial, last)])


def block_lists(rows, count):
    width = rows.shape[-1]
    running = jnp.cumsum(rows, axis=-1)
    ranks = jnp.arange(1, count + 1, dtype=jnp.int32)
    hits = (rows[..., None, :] == 1) & (running[..., None, :] == ranks[:, None])
    columns = jnp.arange(width, dtype=jnp.int32)
    slot_index = jnp.sum(jnp.where(hits, columns, 0), axis=-1)
    slot_valid = jnp.any(hits, axis=-1)
    return (slot_index, slot_valid)


def attend_rows(query_one, key_window, value_window, slot_index, slot_valid, scale):
    key_tiles = key_window[slot_index]
    value_tiles = value_window[slot_index]
    scores = (
        jnp.einsum("rtd,rmud->rtmu", query_one, key_tiles, preferred_element_type=jnp.float32)
        * scale
    )
    scores = jnp.where(slot_valid[:, None, :, None], scores, masked)
    row_top = jnp.max(scores, axis=(2, 3))
    log_total = row_top + jnp.log(jnp.sum(jnp.exp(scores - row_top[:, :, None, None]), axis=(2, 3)))
    weights = jnp.exp(scores - log_total[:, :, None, None])
    weights_b = weights.astype(jnp.bfloat16)
    attended = jnp.einsum(
        "rtmu,rmud->rtd", weights_b, value_tiles, preferred_element_type=jnp.float32
    )
    grad_out = (loss_scale * attended).astype(jnp.bfloat16)
    row_delta = jnp.sum(grad_out.astype(jnp.float32) * attended, axis=2)
    grad_weights = jnp.einsum(
        "rtd,rmud->rtmu", grad_out, value_tiles, preferred_element_type=jnp.float32
    )
    grad_scores = weights * (grad_weights - row_delta[:, :, None, None])
    grad_scores_b = grad_scores.astype(jnp.bfloat16)
    grad_one = (
        jnp.einsum("rtmu,rmud->rtd", grad_scores_b, key_tiles, preferred_element_type=jnp.float32)
        * scale
    ).astype(jnp.bfloat16)
    return (grad_one, grad_out, log_total, row_delta, weights_b, grad_scores_b)


def one_head(query_one, key_win, value_win, slot_index, slot_valid, scale):
    grad_one, grad_out, log_total, row_delta, weights_b, grad_scores_b = attend_rows(
        query_one, key_win, value_win, slot_index, slot_valid, scale
    )
    value_part = jnp.einsum(
        "rtmu,rtd->rmud", weights_b, grad_out, preferred_element_type=jnp.float32
    )
    key_part = (
        jnp.einsum(
            "rtmu,rtd->rmud", grad_scores_b, query_one, preferred_element_type=jnp.float32
        )
        * scale
    )
    slots = key_win.shape[0]
    picks = (slot_index[:, :, None] == jnp.arange(slots, dtype=slot_index.dtype)) & slot_valid[
        :, :, None
    ]
    picks = picks.astype(jnp.float32)
    key_slots = jnp.einsum("rmw,rmud->wud", picks, key_part, precision=lax.Precision.HIGHEST)
    value_slots = jnp.einsum("rmw,rmud->wud", picks, value_part, precision=lax.Precision.HIGHEST)
    return (grad_one, key_slots, value_slots)


def head_kernel(
    idx_ref, valid_ref, q_ref, kw_ref, vw_ref, gq_ref, lo_ref, mid_ref, hi_ref, kacc, vacc, *, scale
):
    kacc[...] = jnp.zeros(kacc.shape, kacc.dtype)
    vacc[...] = jnp.zeros(vacc.shape, vacc.dtype)
    nt = (((1,), (1,)), ((), ()))
    tn = (((0,), (0,)), ((), ()))
    column = lax.broadcasted_iota(jnp.int32, (1, M * BLK), 1) // BLK
    rows = q_ref.shape[1]

    def step(r, carry):
        q = q_ref[0, r]
        slots = [idx_ref[r * M + m] for m in range(M)]
        flags = [valid_ref[r * M + m] > 0 for m in range(M)]
        key_tiles = jnp.concatenate([kw_ref[0, 0, s] for s in slots], axis=0)
        value_tiles = jnp.concatenate([vw_ref[0, 0, s] for s in slots], axis=0)
        usable = column < 0
        for m in range(M):
            usable = usable | ((column == m) & flags[m])
        scores = lax.dot_general(q, key_tiles, nt, preferred_element_type=jnp.float32) * scale
        scores = jnp.where(usable, scores, masked)
        top = scores.max(axis=1, keepdims=True)
        log_total = top + jnp.log(jnp.exp(scores - top).sum(axis=1, keepdims=True))
        weights = jnp.exp(scores - log_total)
        weights_b = weights.astype(jnp.bfloat16)
        attended = jnp.dot(weights_b, value_tiles, preferred_element_type=jnp.float32)
        grad_out = (loss_scale * attended).astype(jnp.bfloat16)
        row_delta = (grad_out.astype(jnp.float32) * attended).sum(axis=1, keepdims=True)
        grad_w = lax.dot_general(grad_out, value_tiles, nt, preferred_element_type=jnp.float32)
        grad_s = (weights * (grad_w - row_delta)).astype(jnp.bfloat16)
        grad_q = jnp.dot(grad_s, key_tiles, preferred_element_type=jnp.float32)
        key_part = lax.dot_general(grad_s, q, tn, preferred_element_type=jnp.float32) * scale
        value_part = lax.dot_general(weights_b, grad_out, tn, preferred_element_type=jnp.float32)
        for m in range(M):
            keep = jnp.where(flags[m], 1.0, 0.0)
            kacc[slots[m]] = kacc[slots[m]] + key_part[m * BLK : (m + 1) * BLK] * keep
            vacc[slots[m]] = vacc[slots[m]] + value_part[m * BLK : (m + 1) * BLK] * keep
        gq_ref[r, 0] = (grad_q * scale).astype(gq_ref.dtype)
        return carry

    lax.fori_loop(0, rows, step, 0, unroll=True)
    lo_ref[0, 0] = kacc[0:rows].astype(lo_ref.dtype)
    lo_ref[1, 0] = vacc[0:rows].astype(lo_ref.dtype)
    mid_ref[0, 0] = kacc[rows : 2 * rows]
    mid_ref[1, 0] = vacc[rows : 2 * rows]
    hi_ref[0, 0] = kacc[2 * rows : 3 * rows].astype(hi_ref.dtype)
    hi_ref[1, 0] = vacc[2 * rows : 3 * rows].astype(hi_ref.dtype)


def head_call(query_blocks, window, slot_index, slot_valid, scale):
    heads, rows = query_blocks.shape[:2]
    width = window.shape[2]
    idx = slot_index.reshape(-1).astype(jnp.int32)
    val = slot_valid.reshape(-1).astype(jnp.int32)
    own = lambda h, i, v: (h, 0, 0, 0)
    keys_of = lambda h, i, v: (0, h, 0, 0, 0)
    values_of = lambda h, i, v: (1, h, 0, 0, 0)
    edges = pl.BlockSpec((2, 1, rows, BLK, HD), keys_of)
    spec = pltpu.PrefetchScalarGridSpec(
        num_scalar_prefetch=2,
        grid=(heads,),
        in_specs=[
            pl.BlockSpec((1, rows, BLK, HD), own),
            pl.BlockSpec((1, 1, width, BLK, HD), keys_of),
            pl.BlockSpec((1, 1, width, BLK, HD), values_of),
        ],
        out_specs=[pl.BlockSpec((rows, 1, BLK, HD), lambda h, i, v: (0, h, 0, 0)), edges, edges, edges],
        scratch_shapes=[
            pltpu.VMEM((width, BLK, HD), jnp.float32),
            pltpu.VMEM((width, BLK, HD), jnp.float32),
        ],
    )
    return pl.pallas_call(
        functools.partial(head_kernel, scale=scale),
        grid_spec=spec,
        out_shape=[
            jax.ShapeDtypeStruct((rows, heads, BLK, HD), jnp.bfloat16),
            jax.ShapeDtypeStruct((2, heads, rows, BLK, HD), jnp.bfloat16),
            jax.ShapeDtypeStruct((2, heads, rows, BLK, HD), jnp.float32),
            jax.ShapeDtypeStruct((2, heads, rows, BLK, HD), jnp.bfloat16),
        ],
        compiler_params=pltpu.CompilerParams(dimension_semantics=("arbitrary",)),
    )(idx, val, query_blocks, window, window)


def body(query, keys, values, block_mask):
    scale = HD ** (-0.5)
    tokens_here = query.shape[0]
    heads_all = query.shape[1] // HD
    spread = lax.axis_size("uly")
    heads_here = heads_all // spread
    group_tokens = tokens_here * spread
    group_blocks = group_tokens // BLK
    position = lax.axis_index("blk")
    padded_mask = jnp.pad(block_mask, ((0, 0), (group_blocks, group_blocks)))
    window_mask = lax.dynamic_slice_in_dim(
        padded_mask, position * group_blocks, 3 * group_blocks, 1
    )
    slot_index, slot_valid = block_lists(window_mask, M)

    def heads_major(array):
        split = array.reshape(tokens_here, spread, heads_here, HD)
        return jnp.transpose(split, (2, 1, 0, 3))

    pair = jnp.stack([heads_major(keys), heads_major(values)])
    pair = lax.all_to_all(pair, "uly", split_axis=2, concat_axis=2, tiled=True)
    pair = pair.reshape(2, heads_here, group_tokens, HD)
    beside = padded(pair, (("blk", 2),), group_tokens)
    query_got = lax.all_to_all(heads_major(query), "uly", split_axis=1, concat_axis=1, tiled=True)
    window = beside.reshape(2, heads_here, 3 * group_blocks, BLK, HD)
    query_blocks = query_got.reshape(heads_here, group_blocks, BLK, HD)
    grad_one, lower, middle, upper = head_call(
        query_blocks, window, slot_index, slot_valid, scale
    )
    from_upper = from_behind(lower.reshape(2, heads_here, group_tokens, HD), "blk", -1)
    from_lower = from_behind(upper.reshape(2, heads_here, group_tokens, HD), "blk", 1)
    back_query = lax.all_to_all(grad_one, "uly", split_axis=0, concat_axis=0, tiled=True)
    totals = (
        middle.reshape(2, heads_here, group_tokens, HD)
        + from_upper.astype(jnp.float32)
        + from_lower.astype(jnp.float32)
    )
    grads = totals.astype(jnp.bfloat16).reshape(2, heads_here, spread, tokens_here, HD)
    back = lax.all_to_all(grads, "uly", split_axis=2, concat_axis=2, tiled=True)
    back_query = jnp.transpose(back_query, (2, 0, 1, 3)).reshape(tokens_here, heads_all * HD)
    back = jnp.transpose(back, (0, 3, 2, 1, 4)).reshape(2, tokens_here, heads_all * HD)
    return (back_query, back[0], back[1])


def solution(mesh):
    in_specs = (
        P(("blk", "uly"), None),
        P(("blk", "uly"), None),
        P(("blk", "uly"), None),
        P("blk", None),
    )
    out_specs = (P(("blk", "uly"), None), P(("blk", "uly"), None), P(("blk", "uly"), None))
    return jax.shard_map(body, mesh=mesh, in_specs=in_specs, out_specs=out_specs, check_vma=False)
```
